256 devices in a mesh: seq: 32 (over x, z), tensor: 8 (over y, core).
Axes of the slice: x: 4, y: 4, z: 8, core: 2. Of those that a mesh axis runs over, the one named last changes fastest.
Arguments:
- features: bfloat16 [16, 7168], P(None, 'seq'), may hold values from -300 to 300
- input_norm_scale: float32 [7168], P('seq'), may hold values from 0.25 to 1.75
- query_key_value_weight: bfloat16 [7168, 3, 7168], P('seq', None, 'tensor'), may hold values from -0.0625 to 0.0625
- adapter_down_weight: bfloat16 [7168, 128], P('seq'), may hold values from -0.0625 to 0.0625
- adapter_up_weight: bfloat16 [128, 7168], P(None, 'tensor'), may hold values from -0.5 to 0.5
- output_weight: bfloat16 [7168, 3584], P('tensor', 'seq'), may hold values from -0.0625 to 0.0625
- cached_key_rows: bfloat16 [4, 16384, 7168], P(None, 'seq', 'tensor'), may hold values from -400 to 400
- cached_value_rows: bfloat16 [4, 16384, 7168], P(None, 'seq', 'tensor'), may hold values from -6 to 6
- lengths: int32 [4], replicated, may hold values from 16 to 16380, as said below
- sinks: int32 [4], replicated, may hold values from 1 to 4, as said below
- windows: int32 [4], replicated, may hold values from 2048 to 4096, as said below
Outputs:
- mixed: float32 [16, 3584], P(None, 'seq')
- new_kv: float32 [2, 16, 7168], P(None, None, 'tensor')
The draws below stay inside these ranges and needn't reach their ends.
Inputs may be any that keep to these rules, and one draw needn't show every extreme that they name: `lengths`: heavy-tailed; at least one request has 16380. `sinks`: at least one request has 4. `windows`: at least one request has 4096.
All inputs are finite; a program needn't handle non-finite values.
Results may differ from the reference program's by a relative error of at most 0.022.
Values sent between devices are 32-bit elements; how exact they have to be, the bound alone decides.
No kernel may reach another device: no remote copies, remote signals or barrier semaphores. Data moves between devices by JAX's collectives and lax.ppermute only.
A program may use at most 64 MiB of HBM per device.

```python
import math
import jax
import jax.numpy as jnp
from jax import lax

D = 3584
HEADS = 32
HD = 224
ADAPTER_RANK = 128
REQ = 4
NEW = 4
SINKS = 4
INPUT_WIDTH = 7168
ATTENTION_WIDTH = 7168
CTX = 16384
WINDOW = 4096
ROWS = 16


def lengths_common(key):
    sub = jax.random.fold_in(key, 11)
    first, second, third = jax.random.split(sub, 3)
    power = jax.random.randint(first, (REQ,), 4, int(math.log2(CTX)), dtype=jnp.int32)
    base = jnp.left_shift(jnp.ones((REQ,), jnp.int32), power)
    extra = jax.random.randint(second, (REQ,), 0, base, dtype=jnp.int32)
    longest = CTX - NEW
    length = jnp.minimum(base + extra, longest)
    forced = jax.random.randint(third, (), 0, REQ, dtype=jnp.int32)
    return jnp.where(jnp.arange(REQ, dtype=jnp.int32) == forced, longest, length).astype(jnp.int32)


def draw_lengths(key, part):
    return lengths_common(key)


def draw_sinks(key, part):
    first, second = jax.random.split(jax.random.fold_in(key, 12))
    count = jax.random.randint(first, (REQ,), 1, SINKS + 1, dtype=jnp.int32)
    forced = jax.random.randint(second, (), 0, REQ, dtype=jnp.int32)
    return jnp.where(jnp.arange(REQ, dtype=jnp.int32) == forced, SINKS, count).astype(jnp.int32)


def draw_windows(key, part):
    first, second = jax.random.split(jax.random.fold_in(key, 13))
    lowest = max(NEW + 2, WINDOW // 2)
    width = jax.random.randint(first, (REQ,), lowest, WINDOW + 1, dtype=jnp.int32)
    forced = jax.random.randint(second, (), 0, REQ, dtype=jnp.int32)
    return jnp.where(jnp.arange(REQ, dtype=jnp.int32) == forced, WINDOW, width).astype(jnp.int32)


def draw_cached_key_rows(key, part):
    sub = jax.random.fold_in(key, 21)
    position = jnp.arange(CTX, dtype=jnp.int32)
    lift = jnp.where(position < SINKS, 1.6, 1.0)[:, None]

    def one(index):
        inner = jax.random.fold_in(sub, index)
        base = jnp.clip(jax.random.normal(inner, (CTX, ATTENTION_WIDTH)), -6.0, 6.0) * 1.8 * lift
        return base.astype(jnp.bfloat16)
    return lax.map(one, jnp.arange(REQ, dtype=jnp.int32))


def draw_features(key, part):
    first, second, third = jax.random.split(jax.random.fold_in(key, 31), 3)
    column = jnp.arange(INPUT_WIDTH, dtype=jnp.float32)
    rising = jnp.exp(0.5 * math.log(3.0) * column / INPUT_WIDTH)
    col_scale = rising * jnp.exp(jax.random.uniform(first, (INPUT_WIDTH,), minval=0.0, maxval=math.log(10.0)))
    row_scale = jnp.exp(jax.random.uniform(second, (ROWS,), minval=math.log(0.3), maxval=math.log(3.0)))
    base = jnp.clip(jax.random.normal(third, (ROWS, INPUT_WIDTH)), -4.0, 4.0)
    return (base * row_scale[:, None] * col_scale[None, :]).astype(jnp.bfloat16)


def level_of(stream_key, dims, cuts, low, high):
    gain = 1.0
    for dim, shards_of in cuts:
        draws = jax.random.uniform(jax.random.fold_in(jax.random.fold_in(stream_key, 6), dim), (shards_of,), jnp.float32, low / len(cuts), high / len(cuts))
        gain = gain * jnp.repeat(jnp.exp(draws), dims[dim] // shards_of).reshape((-1,) + (1,) * (len(dims) - 1 - dim))
    return gain


def gaussian(rng, shape, spread, bound, pieces=(), held_as=jnp.bfloat16):
    gain = level_of(rng, shape, pieces, -0.22, 0.18) if pieces else 1.0
    values = jax.random.normal(rng, shape, jnp.float32) * spread * gain
    return jnp.minimum(jnp.maximum(values, -bound), bound).astype(held_as)


def setup_inputs(seed: int = 0) -> dict:
    key_of = jax.random.split(jax.random.key(seed), 12)
    features = draw_features(jax.random.fold_in(key_of[11], 71), 0)
    input_norm_scale = jnp.clip(1.0 + 0.15 * jax.random.normal(key_of[1], (INPUT_WIDTH,), jnp.float32), 0.25, 1.75)
    query_key_value_weight = gaussian(key_of[2], (INPUT_WIDTH, 3, ATTENTION_WIDTH), INPUT_WIDTH ** -0.5, 0.0625, ((0, 32), (2, 8)))
    adapter_down_weight = gaussian(key_of[3], (INPUT_WIDTH, ADAPTER_RANK), INPUT_WIDTH ** -0.5, 0.0625, ((0, 32),))
    adapter_up_weight = gaussian(key_of[4], (ADAPTER_RANK, ATTENTION_WIDTH), ADAPTER_RANK ** -0.5, 0.5, ((1, 8),))
    output_weight = gaussian(key_of[5], (ATTENTION_WIDTH, D), ATTENTION_WIDTH ** -0.5, 0.0625, ((0, 8), (1, 32)))
    cached_key_rows = draw_cached_key_rows(jax.random.fold_in(key_of[11], 71), 0)
    cached_value_rows = gaussian(key_of[7], (REQ, CTX, ATTENTION_WIDTH), 1.0, 6.0, ((1, 32), (2, 8)))
    lengths = draw_lengths(jax.random.fold_in(key_of[11], 71), 0)
    sinks = draw_sinks(jax.random.fold_in(key_of[11], 71), 0)
    windows = draw_windows(jax.random.fold_in(key_of[11], 71), 0)
    return dict(features=features, input_norm_scale=input_norm_scale, query_key_value_weight=query_key_value_weight, adapter_down_weight=adapter_down_weight, adapter_up_weight=adapter_up_weight, output_weight=output_weight, cached_key_rows=cached_key_rows, cached_value_rows=cached_value_rows, lengths=lengths, sinks=sinks, windows=windows)


NEG = -1e+30
CUT = -1e+29

def reference(features, input_norm_scale, query_key_value_weight, adapter_down_weight, adapter_up_weight, output_weight, cached_key_rows, cached_value_rows, lengths, sinks, windows):
    feat = features.astype(jnp.float32)
    mean_sq = lax.optimization_barrier(jnp.sum(feat * feat, axis=1)) / INPUT_WIDTH
    scale_rows = lax.rsqrt(mean_sq + 1e-05)[:, None]
    scaled_scores = (feat * input_norm_scale).astype(jnp.bfloat16)
    projected = jnp.dot(scaled_scores, query_key_value_weight.reshape(INPUT_WIDTH, 3 * ATTENTION_WIDTH), preferred_element_type=jnp.float32)
    low_rank_query = (jnp.dot(scaled_scores, adapter_down_weight, preferred_element_type=jnp.float32) * scale_rows).astype(jnp.bfloat16)
    query_adapter = jnp.dot(low_rank_query, adapter_up_weight, preferred_element_type=jnp.float32)
    queries = (projected[:, :ATTENTION_WIDTH] * scale_rows + query_adapter).astype(jnp.bfloat16)
    keys_full = projected[:, ATTENTION_WIDTH:2 * ATTENTION_WIDTH] * scale_rows
    values_full = projected[:, 2 * ATTENTION_WIDTH:] * scale_rows
    new_keys = keys_full.astype(jnp.bfloat16)
    new_values = values_full.astype(jnp.bfloat16)
    query_all = queries.astype(jnp.float32).reshape(REQ, NEW, HEADS, HD)
    key_all = new_keys.astype(jnp.float32).reshape(REQ, NEW, HEADS, HD)
    value_all = new_values.astype(jnp.float32).reshape(REQ, NEW, HEADS, HD)
    position = jnp.arange(CTX, dtype=jnp.int32)
    order = jnp.arange(NEW, dtype=jnp.int32)
    causal = order[:, None] >= order[None, :]

    def one_request(index):
        length = lengths[index]
        sink = sinks[index]
        window = windows[index]
        keys = lax.dynamic_index_in_dim(cached_key_rows, index, 0, False).astype(jnp.float32).reshape(CTX, HEADS, HD)
        values = lax.dynamic_index_in_dim(cached_value_rows, index, 0, False).astype(jnp.float32).reshape(CTX, HEADS, HD)
        query = lax.dynamic_index_in_dim(query_all, index, 0, False)
        own_key = lax.dynamic_index_in_dim(key_all, index, 0, False)
        own_value = lax.dynamic_index_in_dim(value_all, index, 0, False)
        seen = (position[None, :] < length) & ((position[None, :] < sink) | (length + order[:, None] - position[None, :] < window))
        cache_s = jnp.where(seen[None], jnp.einsum('thd,phd->htp', query, keys) * HD ** (-0.5), NEG)
        own_s = jnp.where(causal[None], jnp.einsum('thd,uhd->htu', query, own_key) * HD ** (-0.5), NEG)
        top = jnp.maximum(lax.optimization_barrier(jnp.max(cache_s, axis=-1)), lax.optimization_barrier(jnp.max(own_s, axis=-1)))
        cache_e = jnp.where(cache_s > CUT, jnp.exp(cache_s - top[..., None]), 0.0)
        own_e = jnp.where(own_s > CUT, jnp.exp(own_s - top[..., None]), 0.0)
        total = lax.optimization_barrier(jnp.sum(cache_e, axis=-1)) + lax.optimization_barrier(jnp.sum(own_e, axis=-1))
        combined = jnp.einsum('htp,phd->htd', cache_e.astype(jnp.bfloat16).astype(jnp.float32), values)
        combined = combined + jnp.einsum('htu,uhd->htd', own_e.astype(jnp.bfloat16).astype(jnp.float32), own_value)
        return (combined / total[..., None]).transpose(1, 0, 2).reshape(NEW, ATTENTION_WIDTH)
    attn = lax.map(one_request, jnp.arange(REQ, dtype=jnp.int32)).reshape(ROWS, ATTENTION_WIDTH).astype(jnp.bfloat16)
    mixed = jnp.dot(attn, output_weight, preferred_element_type=jnp.float32)
    return (mixed, jnp.stack([keys_full, values_full]))
```

```python
import jax
import jax.numpy as jnp
from jax import lax
from jax.sharding import PartitionSpec as P

HD = 224
NEW = 4
INPUT_WIDTH = 7168


NEG = -1e30
CUT = -1e29


def butterfly_sum(x, axis, size):
    step = 1
    while step < size:
        x = x + lax.ppermute(x, axis, [(i, i ^ step) for i in range(size)])
        step *= 2
    return x


def merge_softmax(a, b, width, heads):
    top = jnp.maximum(a[:, width + heads : width + 2 * heads], b[:, width + heads : width + 2 * heads])
    sa = jnp.exp(a[:, width + heads : width + 2 * heads] - top)
    sb = jnp.exp(b[:, width + heads : width + 2 * heads] - top)
    values = a[:, :width] * jnp.repeat(sa, HD, axis=1) + b[:, :width] * jnp.repeat(sb, HD, axis=1)
    totals = a[:, width : width + heads] * sa + b[:, width : width + heads] * sb
    pad = a.shape[1] - width - 2 * heads
    return jnp.concatenate([values, totals, top, jnp.zeros((a.shape[0], pad), jnp.float32)], axis=1)


def butterfly_softmax(x, axis, size, width, heads):
    step = 1
    while step < size:
        other = lax.ppermute(x, axis, [(i, i ^ step) for i in range(size)])
        x = merge_softmax(x, other, width, heads)
        step *= 2
    return x


def shards(
    features,
    input_norm_scale,
    query_key_value_weight,
    adapter_down_weight,
    adapter_up_weight,
    output_weight,
    cached_key_rows,
    cached_value_rows,
    lengths,
    sinks,
    windows,
    seq_size,
):
    rows = features.shape[0]
    count, span = cached_key_rows.shape[0], cached_key_rows.shape[1]
    local = adapter_up_weight.shape[1]
    heads = local // HD
    rank = adapter_down_weight.shape[1]
    f32, bf16 = jnp.float32, jnp.bfloat16

    feat = features.astype(f32)
    scaled = (feat * input_norm_scale).astype(bf16)
    weights = query_key_value_weight.reshape(query_key_value_weight.shape[0], 3 * local)
    partial_proj = jnp.dot(scaled, weights, preferred_element_type=f32)
    partial_low = jnp.dot(scaled, adapter_down_weight, preferred_element_type=f32)
    partial_sq = jnp.sum(feat * feat, axis=1, keepdims=True)
    packed = jnp.concatenate(
        [partial_proj, partial_low, partial_sq, jnp.zeros((rows, 127), f32)], axis=1
    )
    summed = butterfly_sum(packed, "seq", seq_size)
    projected = summed[:, : 3 * local]
    low = summed[:, 3 * local : 3 * local + rank]
    total_sq = summed[:, 3 * local + rank]
    scale_rows = lax.rsqrt(total_sq / INPUT_WIDTH + 1e-05)[:, None]
    lowrank = (low * scale_rows).astype(bf16)
    query_adapter = jnp.dot(lowrank, adapter_up_weight, preferred_element_type=f32)
    queries = (projected[:, :local] * scale_rows + query_adapter).astype(bf16)
    keys_full = projected[:, local : 2 * local] * scale_rows
    values_full = projected[:, 2 * local :] * scale_rows
    new_keys = keys_full.astype(bf16)
    new_values = values_full.astype(bf16)

    col_head = jnp.arange(local, dtype=jnp.int32) // HD
    head_mask = col_head[None, :] == jnp.arange(heads, dtype=jnp.int32)[:, None]
    q_rows = queries.reshape(count, NEW, local)
    q_block = jnp.where(head_mask[None, :, None, :], q_rows[:, None, :, :], jnp.zeros((), bf16))
    q_block = q_block.reshape(count, heads * NEW, local)
    raw = jnp.einsum(
        "rnc,rpc->rnp", q_block, cached_key_rows, preferred_element_type=f32
    ) * HD ** (-0.5)
    base = lax.axis_index("seq") * span
    position = base + jnp.arange(span, dtype=jnp.int32)
    order = jnp.arange(NEW, dtype=jnp.int32)
    length = lengths[:, None, None]
    sink = sinks[:, None, None]
    window = windows[:, None, None]
    pos = position[None, None, :]
    seen = (pos < length) & ((pos < sink) | (length + order[None, :, None] - pos < window))
    seen = jnp.broadcast_to(seen[:, None], (count, heads, NEW, span)).reshape(count, heads * NEW, span)
    scores = jnp.where(seen, raw, NEG)
    local_top = jnp.max(scores, axis=-1)
    expo = jnp.where(scores > CUT, jnp.exp(scores - local_top[..., None]), 0.0)
    local_total = jnp.sum(expo, axis=-1)
    weighted = jnp.einsum(
        "rnp,rpc->rnc", expo.astype(bf16), cached_value_rows, preferred_element_type=f32
    )
    weighted = jnp.sum(
        jnp.where(head_mask[None, :, None, :], weighted.reshape(count, heads, NEW, local), 0.0),
        axis=1,
    )

    def by_row(x):
        return x.reshape(count, heads, NEW).transpose(0, 2, 1).reshape(rows, heads)

    packed = jnp.concatenate(
        [
            weighted.reshape(rows, local),
            by_row(local_total),
            by_row(local_top),
            jnp.zeros((rows, 128 - 2 * heads), f32),
        ],
        axis=1,
    )
    merged = butterfly_softmax(packed, "seq", seq_size, local, heads)
    cache_out = merged[:, :local]
    cache_total = merged[:, local : local + heads]
    cache_top = merged[:, local + heads : local + 2 * heads]

    query_all = queries.reshape(count, NEW, heads, HD)
    key_all = new_keys.reshape(count, NEW, heads, HD)
    value_all = new_values.reshape(count, NEW, heads, HD)
    fresh = jnp.einsum(
        "rthd,ruhd->rhtu", query_all, key_all, preferred_element_type=f32
    ) * HD ** (-0.5)
    causal = order[:, None] >= order[None, :]
    fresh = jnp.where(causal[None, None], fresh, NEG)
    own_top = by_row(jnp.max(fresh, axis=-1))
    top = jnp.maximum(cache_top, own_top)
    top_rht = top.reshape(count, NEW, heads).transpose(0, 2, 1)
    own_e = jnp.where(fresh > CUT, jnp.exp(fresh - top_rht[..., None]), 0.0)
    own_total = by_row(jnp.sum(own_e, axis=-1))
    own_out = jnp.einsum(
        "rhtu,ruhd->rthd", own_e.astype(bf16), value_all, preferred_element_type=f32
    ).reshape(rows, local)
    cache_scale = jnp.exp(cache_top - top)
    output = cache_out * jnp.repeat(cache_scale, HD, axis=1) + own_out
    total = cache_total * cache_scale + own_total
    attn = (output / jnp.repeat(total, HD, axis=1)).astype(bf16)
    partial_out = jnp.dot(attn, output_weight, preferred_element_type=f32)
    mixed = lax.psum(partial_out, "tensor")
    return (mixed, jnp.stack([keys_full, values_full]))


def solution(mesh):
    in_specs = (
        P(None, "seq"),
        P("seq"),
        P("seq", None, "tensor"),
        P("seq", None),
        P(None, "tensor"),
        P("tensor", "seq"),
        P(None, "seq", "tensor"),
        P(None, "seq", "tensor"),
        P(),
        P(),
        P(),
    )
    out_specs = (P(None, "seq"), P(None, None, "tensor"))
    seq_size = mesh.shape["seq"]

    def body(*args):
        return shards(*args, seq_size)

    return jax.shard_map(body, mesh=mesh, in_specs=in_specs, out_specs=out_specs, check_vma=False)
```

```python
import jax
import jax.numpy as jnp
from jax import lax
from jax.sharding import PartitionSpec as P

HD = 224
NEW = 4
INPUT_WIDTH = 7168


NEG = -1e30
CUT = -1e29


def butterfly_sum(x, axis, size):
    step = 1
    while step < size:
        x = x + lax.ppermute(x, axis, [(i, i ^ step) for i in range(size)])
        step *= 2
    return x


def merge_softmax(a, b, width, heads):
    top = jnp.maximum(a[:, width + heads : width + 2 * heads], b[:, width + heads : width + 2 * heads])
    sa = jnp.exp(a[:, width + heads : width + 2 * heads] - top)
    sb = jnp.exp(b[:, width + heads : width + 2 * heads] - top)
    values = a[:, :width] * jnp.repeat(sa, HD, axis=1) + b[:, :width] * jnp.repeat(sb, HD, axis=1)
    totals = a[:, width : width + heads] * sa + b[:, width : width + heads] * sb
    pad = a.shape[1] - width - 2 * heads
    return jnp.concatenate([values, totals, top, jnp.zeros((a.shape[0], pad), jnp.float32)], axis=1)


def butterfly_softmax(x, axis, size, width, heads):
    step = 1
    while step < size:
        other = lax.ppermute(x, axis, [(i, i ^ step) for i in range(size)])
        x = merge_softmax(x, other, width, heads)
        step *= 2
    return x


def shards(
    features,
    input_norm_scale,
    query_key_value_weight,
    adapter_down_weight,
    adapter_up_weight,
    output_weight,
    cached_key_rows,
    cached_value_rows,
    lengths,
    sinks,
    windows,
    seq_size,
    tensor_size,
):
    rows = features.shape[0]
    count, span = cached_key_rows.shape[0], cached_key_rows.shape[1]
    local = adapter_up_weight.shape[1]
    heads = local // HD
    rank = adapter_down_weight.shape[1]
    f32, bf16 = jnp.float32, jnp.bfloat16

    feat = features.astype(f32)
    scaled = (feat * input_norm_scale).astype(bf16)

    def project(j):
        return jnp.dot(scaled, query_key_value_weight[:, j, :], preferred_element_type=f32)

    partial_low = jnp.dot(scaled, adapter_down_weight, preferred_element_type=f32)
    partial_sq = jnp.sum(feat * feat, axis=1, keepdims=True)
    packed = jnp.concatenate(
        [project(0), partial_low, partial_sq, jnp.zeros((rows, 127), f32)], axis=1
    )
    summed = butterfly_sum(packed, "seq", seq_size)
    kv_summed = butterfly_sum(jnp.concatenate([project(1), project(2)], axis=1), "seq", seq_size)
    low = summed[:, local : local + rank]
    total_sq = summed[:, local + rank]
    scale_rows = lax.rsqrt(total_sq / INPUT_WIDTH + 1e-05)[:, None]
    lowrank = (low * scale_rows).astype(bf16)
    query_adapter = jnp.dot(lowrank, adapter_up_weight, preferred_element_type=f32)
    queries = (summed[:, :local] * scale_rows + query_adapter).astype(bf16)
    keys_full = kv_summed[:, :local] * scale_rows
    values_full = kv_summed[:, local:] * scale_rows
    new_keys = keys_full.astype(bf16)
    new_values = values_full.astype(bf16)

    col_head = jnp.arange(local, dtype=jnp.int32) // HD
    head_mask = col_head[None, :] == jnp.arange(heads, dtype=jnp.int32)[:, None]
    q_rows = queries.reshape(count, NEW, local)
    q_block = jnp.where(head_mask[None, :, None, :], q_rows[:, None, :, :], jnp.zeros((), bf16))
    q_block = q_block.reshape(count, heads * NEW, local)
    raw = jnp.einsum(
        "rnc,rpc->rnp", q_block, cached_key_rows, preferred_element_type=f32
    ) * HD ** (-0.5)
    base = lax.axis_index("seq") * span
    position = base + jnp.arange(span, dtype=jnp.int32)
    order = jnp.arange(NEW, dtype=jnp.int32)
    length = lengths[:, None, None]
    sink = sinks[:, None, None]
    window = windows[:, None, None]
    pos = position[None, None, :]
    seen = (pos < length) & ((pos < sink) | (length + order[None, :, None] - pos < window))
    seen = jnp.broadcast_to(seen[:, None], (count, heads, NEW, span)).reshape(count, heads * NEW, span)
    scores = jnp.where(seen, raw, NEG)
    local_top = jnp.max(scores, axis=-1)
    expo = jnp.where(scores > CUT, jnp.exp(scores - local_top[..., None]), 0.0)
    local_total = jnp.sum(expo, axis=-1)
    weighted = jnp.einsum(
        "rnp,rpc->rnc", expo.astype(bf16), cached_value_rows, preferred_element_type=f32
    )
    weighted = jnp.sum(
        jnp.where(head_mask[None, :, None, :], weighted.reshape(count, heads, NEW, local), 0.0),
        axis=1,
    )

    def by_row(x):
        return x.reshape(count, heads, NEW).transpose(0, 2, 1).reshape(rows, heads)

    packed = jnp.concatenate(
        [
            weighted.reshape(rows, local),
            by_row(local_total),
            by_row(local_top),
            jnp.zeros((rows, 128 - 2 * heads), f32),
        ],
        axis=1,
    )
    merged = butterfly_softmax(packed, "seq", seq_size, local, heads)
    cache_out = merged[:, :local]
    cache_total = merged[:, local : local + heads]
    cache_top = merged[:, local + heads : local + 2 * heads]

    query_all = queries.reshape(count, NEW, heads, HD)
    key_all = new_keys.reshape(count, NEW, heads, HD)
    value_all = new_values.reshape(count, NEW, heads, HD)
    fresh = jnp.einsum(
        "rthd,ruhd->rhtu", query_all, key_all, preferred_element_type=f32
    ) * HD ** (-0.5)
    causal = order[:, None] >= order[None, :]
    fresh = jnp.where(causal[None, None], fresh, NEG)
    own_top = by_row(jnp.max(fresh, axis=-1))
    top = jnp.maximum(cache_top, own_top)
    top_rht = top.reshape(count, NEW, heads).transpose(0, 2, 1)
    own_e = jnp.where(fresh > CUT, jnp.exp(fresh - top_rht[..., None]), 0.0)
    own_total = by_row(jnp.sum(own_e, axis=-1))
    own_out = jnp.einsum(
        "rhtu,ruhd->rthd", own_e.astype(bf16), value_all, preferred_element_type=f32
    ).reshape(rows, local)
    cache_scale = jnp.exp(cache_top - top)
    output = cache_out * jnp.repeat(cache_scale, HD, axis=1) + own_out
    total = cache_total * cache_scale + own_total
    attn = (output / jnp.repeat(total, HD, axis=1)).astype(bf16)
    partial_out = jnp.dot(attn, output_weight, preferred_element_type=f32)
    mixed = butterfly_sum(partial_out, "tensor", tensor_size)
    return (mixed, jnp.stack([keys_full, values_full]))


def solution(mesh):
    in_specs = (
        P(None, "seq"),
        P("seq"),
        P("seq", None, "tensor"),
        P("seq", None),
        P(None, "tensor"),
        P("tensor", "seq"),
        P(None, "seq", "tensor"),
        P(None, "seq", "tensor"),
        P(),
        P(),
        P(),
    )
    out_specs = (P(None, "seq"), P(None, None, "tensor"))
    seq_size, tensor_size = mesh.shape["seq"], mesh.shape["tensor"]

    def body(*args):
        return shards(*args, seq_size, tensor_size)

    return jax.shard_map(body, mesh=mesh, in_specs=in_specs, out_specs=out_specs, check_vma=False)
```

```python
import jax
import jax.numpy as jnp
from jax import lax
from jax.sharding import PartitionSpec as P

HD = 224
NEW = 4
INPUT_WIDTH = 7168


NEG = -1e30
CUT = -1e29


def butterfly_masks(axes):
    masks, shift = [], 0
    for size in reversed(axes):
        bit = 1
        while bit < size:
            masks.append((bit if 2 * bit < size or size <= 2 else size - 2 if size > 4 else size - 1) << shift)
            bit *= 2
        shift += size.bit_length() - 1
    return masks


def butterfly_sum(x, axis, masks):
    size = 1 << len(masks)
    for mask in masks:
        x = x + lax.ppermute(x, axis, [(i, i ^ mask) for i in range(size)])
    return x


def merge_softmax(a, b, width, heads):
    top = jnp.maximum(a[:, width + heads : width + 2 * heads], b[:, width + heads : width + 2 * heads])
    sa = jnp.exp(a[:, width + heads : width + 2 * heads] - top)
    sb = jnp.exp(b[:, width + heads : width + 2 * heads] - top)
    values = a[:, :width] * jnp.repeat(sa, HD, axis=1) + b[:, :width] * jnp.repeat(sb, HD, axis=1)
    totals = a[:, width : width + heads] * sa + b[:, width : width + heads] * sb
    pad = a.shape[1] - width - 2 * heads
    return jnp.concatenate([values, totals, top, jnp.zeros((a.shape[0], pad), jnp.float32)], axis=1)


def butterfly_softmax(x, axis, masks, width, heads):
    size = 1 << len(masks)
    for mask in masks:
        other = lax.ppermute(x, axis, [(i, i ^ mask) for i in range(size)])
        x = merge_softmax(x, other, width, heads)
    return x


RINGS = {"seq": {32: (4, 8)}, "tensor": {8: (4, 2)}}


def axis_masks(axis, size):
    rings = RINGS[axis].get(size, (size,))
    return butterfly_masks(rings)


def shards(
    features,
    input_norm_scale,
    query_key_value_weight,
    adapter_down_weight,
    adapter_up_weight,
    output_weight,
    cached_key_rows,
    cached_value_rows,
    lengths,
    sinks,
    windows,
    seq_masks,
    tensor_masks,
):
    rows = features.shape[0]
    count, span = cached_key_rows.shape[0], cached_key_rows.shape[1]
    local = adapter_up_weight.shape[1]
    heads = local // HD
    rank = adapter_down_weight.shape[1]
    f32, bf16 = jnp.float32, jnp.bfloat16

    feat = features.astype(f32)
    scaled = (feat * input_norm_scale).astype(bf16)

    def project(j):
        return jnp.dot(scaled, query_key_value_weight[:, j, :], preferred_element_type=f32)

    partial_low = jnp.dot(scaled, adapter_down_weight, preferred_element_type=f32)
    partial_sq = jnp.sum(feat * feat, axis=1, keepdims=True)
    packed = jnp.concatenate(
        [project(0), partial_low, partial_sq, jnp.zeros((rows, 127), f32)], axis=1
    )
    summed = butterfly_sum(packed, "seq", seq_masks)
    kv_summed = butterfly_sum(jnp.concatenate([project(1), project(2)], axis=1), "seq", seq_masks)
    low = summed[:, local : local + rank]
    total_sq = summed[:, local + rank]
    scale_rows = lax.rsqrt(total_sq / INPUT_WIDTH + 1e-05)[:, None]
    lowrank = (low * scale_rows).astype(bf16)
    query_adapter = jnp.dot(lowrank, adapter_up_weight, preferred_element_type=f32)
    queries = (summed[:, :local] * scale_rows + query_adapter).astype(bf16)
    keys_full = kv_summed[:, :local] * scale_rows
    values_full = kv_summed[:, local:] * scale_rows
    new_keys = keys_full.astype(bf16)
    new_values = values_full.astype(bf16)

    col_head = jnp.arange(local, dtype=jnp.int32) // HD
    head_mask = col_head[None, :] == jnp.arange(heads, dtype=jnp.int32)[:, None]
    q_rows = queries.reshape(count, NEW, local)
    q_block = jnp.where(head_mask[None, :, None, :], q_rows[:, None, :, :], jnp.zeros((), bf16))
    q_block = q_block.reshape(count, heads * NEW, local)
    raw = jnp.einsum(
        "rnc,rpc->rnp", q_block, cached_key_rows, preferred_element_type=f32
    ) * HD ** (-0.5)
    base = lax.axis_index("seq") * span
    position = base + jnp.arange(span, dtype=jnp.int32)
    order = jnp.arange(NEW, dtype=jnp.int32)
    length = lengths[:, None, None]
    sink = sinks[:, None, None]
    window = windows[:, None, None]
    pos = position[None, None, :]
    seen = (pos < length) & ((pos < sink) | (length + order[None, :, None] - pos < window))
    seen = jnp.broadcast_to(seen[:, None], (count, heads, NEW, span)).reshape(count, heads * NEW, span)
    scores = jnp.where(seen, raw, NEG)
    local_top = jnp.max(scores, axis=-1)
    expo = jnp.where(scores > CUT, jnp.exp(scores - local_top[..., None]), 0.0)
    local_total = jnp.sum(expo, axis=-1)
    weighted = jnp.einsum(
        "rnp,rpc->rnc", expo.astype(bf16), cached_value_rows, preferred_element_type=f32
    )
    weighted = jnp.sum(
        jnp.where(head_mask[None, :, None, :], weighted.reshape(count, heads, NEW, local), 0.0),
        axis=1,
    )

    def by_row(x):
        return x.reshape(count, heads, NEW).transpose(0, 2, 1).reshape(rows, heads)

    packed = jnp.concatenate(
        [
            weighted.reshape(rows, local),
            by_row(local_total),
            by_row(local_top),
            jnp.zeros((rows, 128 - 2 * heads), f32),
        ],
        axis=1,
    )
    merged = butterfly_softmax(packed, "seq", seq_masks, local, heads)
    cache_out = merged[:, :local]
    cache_total = merged[:, local : local + heads]
    cache_top = merged[:, local + heads : local + 2 * heads]

    query_all = queries.reshape(count, NEW, heads, HD)
    key_all = new_keys.reshape(count, NEW, heads, HD)
    value_all = new_values.reshape(count, NEW, heads, HD)
    fresh = jnp.einsum(
        "rthd,ruhd->rhtu", query_all, key_all, preferred_element_type=f32
    ) * HD ** (-0.5)
    causal = order[:, None] >= order[None, :]
    fresh = jnp.where(causal[None, None], fresh, NEG)
    own_top = by_row(jnp.max(fresh, axis=-1))
    top = jnp.maximum(cache_top, own_top)
    top_rht = top.reshape(count, NEW, heads).transpose(0, 2, 1)
    own_e = jnp.where(fresh > CUT, jnp.exp(fresh - top_rht[..., None]), 0.0)
    own_total = by_row(jnp.sum(own_e, axis=-1))
    own_out = jnp.einsum(
        "rhtu,ruhd->rthd", own_e.astype(bf16), value_all, preferred_element_type=f32
    ).reshape(rows, local)
    cache_scale = jnp.exp(cache_top - top)
    output = cache_out * jnp.repeat(cache_scale, HD, axis=1) + own_out
    total = cache_total * cache_scale + own_total
    attn = (output / jnp.repeat(total, HD, axis=1)).astype(bf16)
    partial_out = jnp.dot(attn, output_weight, preferred_element_type=f32)
    mixed = butterfly_sum(partial_out, "tensor", tensor_masks)
    return (mixed, jnp.stack([keys_full, values_full]))


def solution(mesh):
    in_specs = (
        P(None, "seq"),
        P("seq"),
        P("seq", None, "tensor"),
        P("seq", None),
        P(None, "tensor"),
        P("tensor", "seq"),
        P(None, "seq", "tensor"),
        P(None, "seq", "tensor"),
        P(),
        P(),
        P(),
    )
    out_specs = (P(None, "seq"), P(None, None, "tensor"))
    seq_masks = axis_masks("seq", mesh.shape["seq"])
    tensor_masks = axis_masks("tensor", mesh.shape["tensor"])

    def body(*args):
        return shards(*args, seq_masks, tensor_masks)

    return jax.shard_map(body, mesh=mesh, in_specs=in_specs, out_specs=out_specs, check_vma=False)
```

```python
import jax
import jax.numpy as jnp
from jax import lax
from jax.sharding import PartitionSpec as P

HD = 224
NEW = 4
INPUT_WIDTH = 7168


NEG = -1e30
CUT = -1e29


def butterfly_rounds(axes):
    rounds, shift = [], 0
    for size in reversed(axes):
        masks, bit = [], 1
        while bit < size:
            masks.append((bit if 2 * bit < size or size <= 2 else size - 2 if size > 4 else size - 1) << shift)
            bit *= 2
        rounds += [tuple(masks[i : i + 2]) for i in range(0, len(masks), 2)]
        shift += size.bit_length() - 1
    return rounds


def exchange(x, axis, mask, size):
    return lax.ppermute(x, axis, [(i, i ^ mask) for i in range(size)])


def butterfly_sum(x, axis, rounds):
    size = 1 << sum(len(r) for r in rounds)
    for r in rounds:
        if len(r) == 1:
            x = x + exchange(x, axis, r[0], size)
        else:
            a, b = r
            pa, pb, pc = (exchange(x, axis, m, size) for m in (a, b, a ^ b))
            x = (x + pa) + (pb + pc)
    return x


def merge_softmax(a, b, width, heads):
    top = jnp.maximum(a[:, width + heads : width + 2 * heads], b[:, width + heads : width + 2 * heads])
    sa = jnp.exp(a[:, width + heads : width + 2 * heads] - top)
    sb = jnp.exp(b[:, width + heads : width + 2 * heads] - top)
    values = a[:, :width] * jnp.repeat(sa, HD, axis=1) + b[:, :width] * jnp.repeat(sb, HD, axis=1)
    totals = a[:, width : width + heads] * sa + b[:, width : width + heads] * sb
    pad = a.shape[1] - width - 2 * heads
    return jnp.concatenate([values, totals, top, jnp.zeros((a.shape[0], pad), jnp.float32)], axis=1)


def butterfly_softmax(x, axis, rounds, width, heads):
    size = 1 << sum(len(r) for r in rounds)
    for r in rounds:
        if len(r) == 1:
            x = merge_softmax(x, exchange(x, axis, r[0], size), width, heads)
        else:
            a, b = r
            pa, pb, pc = (exchange(x, axis, m, size) for m in (a, b, a ^ b))
            x = merge_softmax(merge_softmax(x, pa, width, heads), merge_softmax(pb, pc, width, heads), width, heads)
    return x


RINGS = {"seq": {32: (4, 8)}, "tensor": {8: (4, 2)}}


def axis_masks(axis, size):
    rings = RINGS[axis].get(size, (size,))
    return butterfly_rounds(rings)


def shards(
    features,
    input_norm_scale,
    query_key_value_weight,
    adapter_down_weight,
    adapter_up_weight,
    output_weight,
    cached_key_rows,
    cached_value_rows,
    lengths,
    sinks,
    windows,
    seq_masks,
    tensor_masks,
):
    rows = features.shape[0]
    count, span = cached_key_rows.shape[0], cached_key_rows.shape[1]
    local = adapter_up_weight.shape[1]
    heads = local // HD
    rank = adapter_down_weight.shape[1]
    f32, bf16 = jnp.float32, jnp.bfloat16

    feat = features.astype(f32)
    scaled = (feat * input_norm_scale).astype(bf16)

    def project(j):
        return jnp.dot(scaled, query_key_value_weight[:, j, :], preferred_element_type=f32)

    partial_low = jnp.dot(scaled, adapter_down_weight, preferred_element_type=f32)
    partial_sq = jnp.sum(feat * feat, axis=1, keepdims=True)
    packed = jnp.concatenate(
        [project(0), partial_low, partial_sq, jnp.zeros((rows, 127), f32)], axis=1
    )
    summed = butterfly_sum(packed, "seq", seq_masks)
    kv_summed = butterfly_sum(jnp.concatenate([project(1), project(2)], axis=1), "seq", seq_masks)
    low = summed[:, local : local + rank]
    total_sq = summed[:, local + rank]
    scale_rows = lax.rsqrt(total_sq / INPUT_WIDTH + 1e-05)[:, None]
    lowrank = (low * scale_rows).astype(bf16)
    query_adapter = jnp.dot(lowrank, adapter_up_weight, preferred_element_type=f32)
    queries = (summed[:, :local] * scale_rows + query_adapter).astype(bf16)
    keys_full = kv_summed[:, :local] * scale_rows
    values_full = kv_summed[:, local:] * scale_rows
    new_keys = keys_full.astype(bf16)
    new_values = values_full.astype(bf16)

    col_head = jnp.arange(local, dtype=jnp.int32) // HD
    head_mask = col_head[None, :] == jnp.arange(heads, dtype=jnp.int32)[:, None]
    q_rows = queries.reshape(count, NEW, local)
    q_block = jnp.where(head_mask[None, :, None, :], q_rows[:, None, :, :], jnp.zeros((), bf16))
    q_block = q_block.reshape(count, heads * NEW, local)
    raw = jnp.einsum(
        "rnc,rpc->rnp", q_block, cached_key_rows, preferred_element_type=f32
    ) * HD ** (-0.5)
    base = lax.axis_index("seq") * span
    position = base + jnp.arange(span, dtype=jnp.int32)
    order = jnp.arange(NEW, dtype=jnp.int32)
    length = lengths[:, None, None]
    sink = sinks[:, None, None]
    window = windows[:, None, None]
    pos = position[None, None, :]
    seen = (pos < length) & ((pos < sink) | (length + order[None, :, None] - pos < window))
    seen = jnp.broadcast_to(seen[:, None], (count, heads, NEW, span)).reshape(count, heads * NEW, span)
    scores = jnp.where(seen, raw, NEG)
    local_top = jnp.max(scores, axis=-1)
    expo = jnp.where(scores > CUT, jnp.exp(scores - local_top[..., None]), 0.0)
    local_total = jnp.sum(expo, axis=-1)
    weighted = jnp.einsum(
        "rnp,rpc->rnc", expo.astype(bf16), cached_value_rows, preferred_element_type=f32
    )
    weighted = jnp.sum(
        jnp.where(head_mask[None, :, None, :], weighted.reshape(count, heads, NEW, local), 0.0),
        axis=1,
    )

    def by_row(x):
        return x.reshape(count, heads, NEW).transpose(0, 2, 1).reshape(rows, heads)

    packed = jnp.concatenate(
        [
            weighted.reshape(rows, local),
            by_row(local_total),
            by_row(local_top),
            jnp.zeros((rows, 128 - 2 * heads), f32),
        ],
        axis=1,
    )
    merged = butterfly_softmax(packed, "seq", seq_masks, local, heads)
    cache_out = merged[:, :local]
    cache_total = merged[:, local : local + heads]
    cache_top = merged[:, local + heads : local + 2 * heads]

    query_all = queries.reshape(count, NEW, heads, HD)
    key_all = new_keys.reshape(count, NEW, heads, HD)
    value_all = new_values.reshape(count, NEW, heads, HD)
    fresh = jnp.einsum(
        "rthd,ruhd->rhtu", query_all, key_all, preferred_element_type=f32
    ) * HD ** (-0.5)
    causal = order[:, None] >= order[None, :]
    fresh = jnp.where(causal[None, None], fresh, NEG)
    own_top = by_row(jnp.max(fresh, axis=-1))
    top = jnp.maximum(cache_top, own_top)
    top_rht = top.reshape(count, NEW, heads).transpose(0, 2, 1)
    own_e = jnp.where(fresh > CUT, jnp.exp(fresh - top_rht[..., None]), 0.0)
    own_total = by_row(jnp.sum(own_e, axis=-1))
    own_out = jnp.einsum(
        "rhtu,ruhd->rthd", own_e.astype(bf16), value_all, preferred_element_type=f32
    ).reshape(rows, local)
    cache_scale = jnp.exp(cache_top - top)
    output = cache_out * jnp.repeat(cache_scale, HD, axis=1) + own_out
    total = cache_total * cache_scale + own_total
    attn = (output / jnp.repeat(total, HD, axis=1)).astype(bf16)
    partial_out = jnp.dot(attn, output_weight, preferred_element_type=f32)
    mixed = butterfly_sum(partial_out, "tensor", tensor_masks)
    return (mixed, jnp.stack([keys_full, values_full]))


def solution(mesh):
    in_specs = (
        P(None, "seq"),
        P("seq"),
        P("seq", None, "tensor"),
        P("seq", None),
        P(None, "tensor"),
        P("tensor", "seq"),
        P(None, "seq", "tensor"),
        P(None, "seq", "tensor"),
        P(),
        P(),
        P(),
    )
    out_specs = (P(None, "seq"), P(None, None, "tensor"))
    seq_masks = axis_masks("seq", mesh.shape["seq"])
    tensor_masks = axis_masks("tensor", mesh.shape["tensor"])

    def body(*args):
        return shards(*args, seq_masks, tensor_masks)

    return jax.shard_map(body, mesh=mesh, in_specs=in_specs, out_specs=out_specs, check_vma=False)
```

```python
import jax
import jax.numpy as jnp
from jax import lax
from jax.sharding import PartitionSpec as P

HD = 224
NEW = 4
INPUT_WIDTH = 7168


NEG = -1e30
CUT = -1e29


def butterfly_rounds(axes):
    rounds, shift = [], 0
    for size in reversed(axes):
        masks, bit = [], 1
        while bit < size:
            masks.append((bit if 2 * bit < size or size <= 2 else size - 2 if size > 4 else size - 1) << shift)
            bit *= 2
        rounds += [tuple(masks[i : i + 2]) for i in range(0, len(masks), 2)]
        shift += size.bit_length() - 1
    return rounds


def exchange(x, axis, mask, size):
    return lax.ppermute(x, axis, [(i, i ^ mask) for i in range(size)])


def butterfly_sum(x, axis, rounds):
    size = 1 << sum(len(r) for r in rounds)
    for r in rounds:
        if len(r) == 1:
            x = x + exchange(x, axis, r[0], size)
        else:
            a, b = r
            pa, pb, pc = (exchange(x, axis, m, size) for m in (a, b, a ^ b))
            x = (x + pa) + (pb + pc)
    return x


def merge_softmax(a, b, width, heads):
    top = jnp.maximum(a[:, width + heads : width + 2 * heads], b[:, width + heads : width + 2 * heads])
    sa = jnp.exp(a[:, width + heads : width + 2 * heads] - top)
    sb = jnp.exp(b[:, width + heads : width + 2 * heads] - top)
    values = a[:, :width] * jnp.repeat(sa, HD, axis=1) + b[:, :width] * jnp.repeat(sb, HD, axis=1)
    totals = a[:, width : width + heads] * sa + b[:, width : width + heads] * sb
    pad = a.shape[1] - width - 2 * heads
    return jnp.concatenate([values, totals, top, jnp.zeros((a.shape[0], pad), jnp.float32)], axis=1)


def butterfly_softmax(x, axis, rounds, width, heads):
    size = 1 << sum(len(r) for r in rounds)
    for r in rounds:
        if len(r) == 1:
            x = merge_softmax(x, exchange(x, axis, r[0], size), width, heads)
        else:
            a, b = r
            pa, pb, pc = (exchange(x, axis, m, size) for m in (a, b, a ^ b))
            x = merge_softmax(merge_softmax(x, pa, width, heads), merge_softmax(pb, pc, width, heads), width, heads)
    return x


RINGS = {"seq": {32: (4, 8)}, "tensor": {8: (4, 2)}}


def axis_masks(axis, size):
    rings = RINGS[axis].get(size, (size,))
    return butterfly_rounds(rings)


def shards(
    features,
    input_norm_scale,
    query_key_value_weight,
    adapter_down_weight,
    adapter_up_weight,
    output_weight,
    cached_key_rows,
    cached_value_rows,
    lengths,
    sinks,
    windows,
    seq_masks,
    tensor_masks,
):
    rows = features.shape[0]
    count, span = cached_key_rows.shape[0], cached_key_rows.shape[1]
    local = adapter_up_weight.shape[1]
    heads = local // HD
    rank = adapter_down_weight.shape[1]
    f32, bf16 = jnp.float32, jnp.bfloat16

    feat = features.astype(f32)
    scaled = (feat * input_norm_scale).astype(bf16)

    def project(j):
        return jnp.dot(scaled, query_key_value_weight[:, j, :], preferred_element_type=f32)

    partial_low = jnp.dot(scaled, adapter_down_weight, preferred_element_type=f32)
    partial_sq = jnp.sum(feat * feat, axis=1, keepdims=True)
    packed = jnp.concatenate(
        [project(0), partial_low, partial_sq, jnp.zeros((rows, 127), f32)], axis=1
    )
    summed = butterfly_sum(packed, "seq", seq_masks)
    kv_partial, summed = lax.optimization_barrier(
        (jnp.concatenate([project(1), project(2)], axis=1), summed)
    )
    kv_summed = butterfly_sum(kv_partial, "seq", seq_masks)
    low = summed[:, local : local + rank]
    total_sq = summed[:, local + rank]
    scale_rows = lax.rsqrt(total_sq / INPUT_WIDTH + 1e-05)[:, None]
    lowrank = (low * scale_rows).astype(bf16)
    query_adapter = jnp.dot(lowrank, adapter_up_weight, preferred_element_type=f32)
    queries = (summed[:, :local] * scale_rows + query_adapter).astype(bf16)
    keys_full = kv_summed[:, :local] * scale_rows
    values_full = kv_summed[:, local:] * scale_rows
    new_keys = keys_full.astype(bf16)
    new_values = values_full.astype(bf16)

    col_head = jnp.arange(local, dtype=jnp.int32) // HD
    head_mask = col_head[None, :] == jnp.arange(heads, dtype=jnp.int32)[:, None]
    q_rows = queries.reshape(count, NEW, local)
    q_block = jnp.where(head_mask[None, :, None, :], q_rows[:, None, :, :], jnp.zeros((), bf16))
    q_block = q_block.reshape(count, heads * NEW, local)
    raw = jnp.einsum(
        "rnc,rpc->rnp", q_block, cached_key_rows, preferred_element_type=f32
    ) * HD ** (-0.5)
    base = lax.axis_index("seq") * span
    position = base + jnp.arange(span, dtype=jnp.int32)
    order = jnp.arange(NEW, dtype=jnp.int32)
    length = lengths[:, None, None]
    sink = sinks[:, None, None]
    window = windows[:, None, None]
    pos = position[None, None, :]
    seen = (pos < length) & ((pos < sink) | (length + order[None, :, None] - pos < window))
    seen = jnp.broadcast_to(seen[:, None], (count, heads, NEW, span)).reshape(count, heads * NEW, span)
    scores = jnp.where(seen, raw, NEG)
    local_top = jnp.max(scores, axis=-1)
    expo = jnp.where(scores > CUT, jnp.exp(scores - local_top[..., None]), 0.0)
    local_total = jnp.sum(expo, axis=-1)
    weighted = jnp.einsum(
        "rnp,rpc->rnc", expo.astype(bf16), cached_value_rows, preferred_element_type=f32
    )
    weighted = jnp.sum(
        jnp.where(head_mask[None, :, None, :], weighted.reshape(count, heads, NEW, local), 0.0),
        axis=1,
    )

    def by_row(x):
        return x.reshape(count, heads, NEW).transpose(0, 2, 1).reshape(rows, heads)

    packed = jnp.concatenate(
        [
            weighted.reshape(rows, local),
            by_row(local_total),
            by_row(local_top),
            jnp.zeros((rows, 128 - 2 * heads), f32),
        ],
        axis=1,
    )
    merged = butterfly_softmax(packed, "seq", seq_masks, local, heads)
    cache_out = merged[:, :local]
    cache_total = merged[:, local : local + heads]
    cache_top = merged[:, local + heads : local + 2 * heads]

    query_all = queries.reshape(count, NEW, heads, HD)
    key_all = new_keys.reshape(count, NEW, heads, HD)
    value_all = new_values.reshape(count, NEW, heads, HD)
    fresh = jnp.einsum(
        "rthd,ruhd->rhtu", query_all, key_all, preferred_element_type=f32
    ) * HD ** (-0.5)
    causal = order[:, None] >= order[None, :]
    fresh = jnp.where(causal[None, None], fresh, NEG)
    own_top = by_row(jnp.max(fresh, axis=-1))
    top = jnp.maximum(cache_top, own_top)
    top_rht = top.reshape(count, NEW, heads).transpose(0, 2, 1)
    own_e = jnp.where(fresh > CUT, jnp.exp(fresh - top_rht[..., None]), 0.0)
    own_total = by_row(jnp.sum(own_e, axis=-1))
    own_out = jnp.einsum(
        "rhtu,ruhd->rthd", own_e.astype(bf16), value_all, preferred_element_type=f32
    ).reshape(rows, local)
    cache_scale = jnp.exp(cache_top - top)
    output = cache_out * jnp.repeat(cache_scale, HD, axis=1) + own_out
    total = cache_total * cache_scale + own_total
    attn = (output / jnp.repeat(total, HD, axis=1)).astype(bf16)
    partial_out = jnp.dot(attn, output_weight, preferred_element_type=f32)
    mixed = butterfly_sum(partial_out, "tensor", tensor_masks)
    return (mixed, jnp.stack([keys_full, values_full]))


def solution(mesh):
    in_specs = (
        P(None, "seq"),
        P("seq"),
        P("seq", None, "tensor"),
        P("seq", None),
        P(None, "tensor"),
        P("tensor", "seq"),
        P(None, "seq", "tensor"),
        P(None, "seq", "tensor"),
        P(),
        P(),
        P(),
    )
    out_specs = (P(None, "seq"), P(None, None, "tensor"))
    seq_masks = axis_masks("seq", mesh.shape["seq"])
    tensor_masks = axis_masks("tensor", mesh.shape["tensor"])

    def body(*args):
        return shards(*args, seq_masks, tensor_masks)

    return jax.shard_map(body, mesh=mesh, in_specs=in_specs, out_specs=out_specs, check_vma=False)
```

```python
import jax
import jax.numpy as jnp
from jax import lax
from jax.sharding import PartitionSpec as P

HD = 224
NEW = 4
INPUT_WIDTH = 7168


NEG = -1e30
CUT = -1e29


def butterfly_rounds(axes):
    masks, rings, shift = [], [], 0
    for size in reversed(axes):
        bit, ring = 1, []
        while bit < size:
            ring.append((bit if 2 * bit < size or size <= 2 else size - 2 if size > 4 else size - 1) << shift)
            bit *= 2
        rings.append(ring)
        masks += ring
        shift += size.bit_length() - 1
    duals = [
        next(c for c in range(1 << len(masks)) if all(bin(c & m).count("1") % 2 == (j == k) for k, m in enumerate(masks)))
        for j in range(len(masks))
    ]
    pairs = dict(zip(masks, duals))
    return [tuple((m, pairs[m]) for m in ring[i : i + 2]) for ring in rings for i in range(0, len(ring), 2)]


def exchange(x, axis, mask, size):
    return lax.ppermute(x, axis, [(i, i ^ mask) for i in range(size)])


def partners(r):
    if len(r) == 1:
        return [(r[0][0], 1)]
    a, b = r[0][0], r[1][0]
    return [(a, 1), (b, 2), (a ^ b, 3)]


def digit_of(index, r):
    return sum((lax.population_count(index & c) & 1) << k for k, (_, c) in enumerate(r))


def pieces(x, n):
    w = x.shape[1] // n
    return [x[:, j * w : (j + 1) * w] for j in range(n)]


def butterfly_sum(x, axis, rounds, spread=None):
    size = 1 << sum(len(r) for r in rounds)
    index = lax.axis_index(axis)
    width = x.shape[1]
    for r in rounds:
        ways = partners(r)
        digit = digit_of(index, r)
        if spread is not None:
            parts = pieces(spread, 2 ** len(r))
            mine = lax.select_n(digit, *parts)
            got = [
                exchange(jnp.concatenate([x, lax.select_n(digit ^ d, *parts)], axis=1), axis, m, size)
                for m, d in ways
            ]
            recv = [g[:, :width] for g in got]
            bits = [g[:, width:] for g in got]
        else:
            recv = [exchange(x, axis, m, size) for m, _ in ways]
        if len(r) == 1:
            x = x + recv[0]
            if spread is not None:
                spread = mine + bits[0]
        else:
            x = (x + recv[0]) + (recv[1] + recv[2])
            if spread is not None:
                spread = (mine + bits[0]) + (bits[1] + bits[2])
    return x, spread


def merge_softmax(a, b, width, heads):
    top = jnp.maximum(a[:, width + heads : width + 2 * heads], b[:, width + heads : width + 2 * heads])
    sa = jnp.exp(a[:, width + heads : width + 2 * heads] - top)
    sb = jnp.exp(b[:, width + heads : width + 2 * heads] - top)
    values = a[:, :width] * jnp.repeat(sa, HD, axis=1) + b[:, :width] * jnp.repeat(sb, HD, axis=1)
    totals = a[:, width : width + heads] * sa + b[:, width : width + heads] * sb
    pad = a.shape[1] - width - 2 * heads
    return jnp.concatenate([values, totals, top, jnp.zeros((a.shape[0], pad), jnp.float32)], axis=1)


def butterfly_softmax(x, axis, rounds, width, heads, gather):
    size = 1 << sum(len(r) for r in rounds)
    index = lax.axis_index(axis)
    full = x.shape[1]
    for r in reversed(rounds):
        ways = partners(r)
        digit = digit_of(index, r)
        got = [exchange(jnp.concatenate([x, gather], axis=1), axis, m, size) for m, _ in ways]
        recv = [g[:, :full] for g in got]
        by_diff = [gather] + [g[:, full:] for g in got]
        order = [0] + [d for _, d in ways]
        slots = [by_diff[order.index(d)] for d in range(2 ** len(r))]
        gather = jnp.concatenate([lax.select_n(digit ^ j, *slots) for j in range(2 ** len(r))], axis=1)
        if len(r) == 1:
            x = merge_softmax(x, recv[0], width, heads)
        else:
            x = merge_softmax(
                merge_softmax(x, recv[0], width, heads), merge_softmax(recv[1], recv[2], width, heads), width, heads
            )
    return x, gather


RINGS = {"seq": {32: (4, 8)}, "tensor": {8: (4, 2)}}


def axis_masks(axis, size):
    rings = RINGS[axis].get(size, (size,))
    return butterfly_rounds(rings)


def shards(
    features,
    input_norm_scale,
    query_key_value_weight,
    adapter_down_weight,
    adapter_up_weight,
    output_weight,
    cached_key_rows,
    cached_value_rows,
    lengths,
    sinks,
    windows,
    seq_masks,
    tensor_masks,
):
    rows = features.shape[0]
    count, span = cached_key_rows.shape[0], cached_key_rows.shape[1]
    local = adapter_up_weight.shape[1]
    heads = local // HD
    rank = adapter_down_weight.shape[1]
    f32, bf16 = jnp.float32, jnp.bfloat16

    feat = features.astype(f32)
    scaled = (feat * input_norm_scale).astype(bf16)

    def project(j):
        return jnp.dot(scaled, query_key_value_weight[:, j, :], preferred_element_type=f32)

    partial_low = jnp.dot(scaled, adapter_down_weight, preferred_element_type=f32)
    partial_sq = jnp.sum(feat * feat, axis=1, keepdims=True)
    packed = jnp.concatenate(
        [project(0), partial_low, partial_sq, jnp.zeros((rows, 127), f32)], axis=1
    )
    summed, kv_piece = butterfly_sum(
        packed, "seq", seq_masks, jnp.concatenate([project(1), project(2)], axis=1)
    )
    low = summed[:, local : local + rank]
    total_sq = summed[:, local + rank]
    scale_rows = lax.rsqrt(total_sq / INPUT_WIDTH + 1e-05)[:, None]
    lowrank = (low * scale_rows).astype(bf16)
    query_adapter = jnp.dot(lowrank, adapter_up_weight, preferred_element_type=f32)
    queries = (summed[:, :local] * scale_rows + query_adapter).astype(bf16)

    col_head = jnp.arange(local, dtype=jnp.int32) // HD
    head_mask = col_head[None, :] == jnp.arange(heads, dtype=jnp.int32)[:, None]
    q_rows = queries.reshape(count, NEW, local)
    q_block = jnp.where(head_mask[None, :, None, :], q_rows[:, None, :, :], jnp.zeros((), bf16))
    q_block = q_block.reshape(count, heads * NEW, local)
    raw = jnp.einsum(
        "rnc,rpc->rnp", q_block, cached_key_rows, preferred_element_type=f32
    ) * HD ** (-0.5)
    base = lax.axis_index("seq") * span
    position = base + jnp.arange(span, dtype=jnp.int32)
    order = jnp.arange(NEW, dtype=jnp.int32)
    length = lengths[:, None, None]
    sink = sinks[:, None, None]
    window = windows[:, None, None]
    pos = position[None, None, :]
    seen = (pos < length) & ((pos < sink) | (length + order[None, :, None] - pos < window))
    seen = jnp.broadcast_to(seen[:, None], (count, heads, NEW, span)).reshape(count, heads * NEW, span)
    scores = jnp.where(seen, raw, NEG)
    local_top = jnp.max(scores, axis=-1)
    expo = jnp.where(scores > CUT, jnp.exp(scores - local_top[..., None]), 0.0)
    local_total = jnp.sum(expo, axis=-1)
    weighted = jnp.einsum(
        "rnp,rpc->rnc", expo.astype(bf16), cached_value_rows, preferred_element_type=f32
    )
    weighted = jnp.sum(
        jnp.where(head_mask[None, :, None, :], weighted.reshape(count, heads, NEW, local), 0.0),
        axis=1,
    )

    def by_row(x):
        return x.reshape(count, heads, NEW).transpose(0, 2, 1).reshape(rows, heads)

    packed = jnp.concatenate(
        [
            weighted.reshape(rows, local),
            by_row(local_total),
            by_row(local_top),
            jnp.zeros((rows, 128 - 2 * heads), f32),
        ],
        axis=1,
    )
    merged, kv_summed = butterfly_softmax(packed, "seq", seq_masks, local, heads, kv_piece)
    keys_full = kv_summed[:, :local] * scale_rows
    values_full = kv_summed[:, local:] * scale_rows
    new_keys = keys_full.astype(bf16)
    new_values = values_full.astype(bf16)
    cache_out = merged[:, :local]
    cache_total = merged[:, local : local + heads]
    cache_top = merged[:, local + heads : local + 2 * heads]

    query_all = queries.reshape(count, NEW, heads, HD)
    key_all = new_keys.reshape(count, NEW, heads, HD)
    value_all = new_values.reshape(count, NEW, heads, HD)
    fresh = jnp.einsum(
        "rthd,ruhd->rhtu", query_all, key_all, preferred_element_type=f32
    ) * HD ** (-0.5)
    causal = order[:, None] >= order[None, :]
    fresh = jnp.where(causal[None, None], fresh, NEG)
    own_top = by_row(jnp.max(fresh, axis=-1))
    top = jnp.maximum(cache_top, own_top)
    top_rht = top.reshape(count, NEW, heads).transpose(0, 2, 1)
    own_e = jnp.where(fresh > CUT, jnp.exp(fresh - top_rht[..., None]), 0.0)
    own_total = by_row(jnp.sum(own_e, axis=-1))
    own_out = jnp.einsum(
        "rhtu,ruhd->rthd", own_e.astype(bf16), value_all, preferred_element_type=f32
    ).reshape(rows, local)
    cache_scale = jnp.exp(cache_top - top)
    output = cache_out * jnp.repeat(cache_scale, HD, axis=1) + own_out
    total = cache_total * cache_scale + own_total
    attn = (output / jnp.repeat(total, HD, axis=1)).astype(bf16)
    partial_out = jnp.dot(attn, output_weight, preferred_element_type=f32)
    mixed, _ = butterfly_sum(partial_out, "tensor", tensor_masks)
    return (mixed, jnp.stack([keys_full, values_full]))


def solution(mesh):
    in_specs = (
        P(None, "seq"),
        P("seq"),
        P("seq", None, "tensor"),
        P("seq", None),
        P(None, "tensor"),
        P("tensor", "seq"),
        P(None, "seq", "tensor"),
        P(None, "seq", "tensor"),
        P(),
        P(),
        P(),
    )
    out_specs = (P(None, "seq"), P(None, None, "tensor"))
    seq_masks = axis_masks("seq", mesh.shape["seq"])
    tensor_masks = axis_masks("tensor", mesh.shape["tensor"])

    def body(*args):
        return shards(*args, seq_masks, tensor_masks)

    return jax.shard_map(body, mesh=mesh, in_specs=in_specs, out_specs=out_specs, check_vma=False)
```

```python
import jax
import jax.numpy as jnp
from jax import lax
from jax.sharding import PartitionSpec as P

HD = 224
NEW = 4
INPUT_WIDTH = 7168


NEG = -1e30
CUT = -1e29


def butterfly_rounds(axes):
    rounds, shift = [], 0
    for size in reversed(axes):
        masks, bit = [], 1
        while bit < size:
            masks.append((bit if 2 * bit < size or size <= 2 else size - 2 if size > 4 else size - 1) << shift)
            bit *= 2
        rounds += [tuple(masks[i : i + 2]) for i in range(0, len(masks), 2)]
        shift += size.bit_length() - 1
    return rounds


def exchange(x, axis, mask, size):
    return lax.ppermute(x, axis, [(i, i ^ mask) for i in range(size)])


def butterfly_sum(x, axis, rounds):
    size = 1 << sum(len(r) for r in rounds)
    for r in rounds:
        if len(r) == 1:
            x = x + exchange(x, axis, r[0], size)
        else:
            a, b = r
            pa, pb, pc = (exchange(x, axis, m, size) for m in (a, b, a ^ b))
            x = (x + pa) + (pb + pc)
    return x


def merge_softmax(a, b, width, heads):
    top = jnp.maximum(a[:, width + heads : width + 2 * heads], b[:, width + heads : width + 2 * heads])
    sa = jnp.exp(a[:, width + heads : width + 2 * heads] - top)
    sb = jnp.exp(b[:, width + heads : width + 2 * heads] - top)
    values = a[:, :width] * jnp.repeat(sa, HD, axis=1) + b[:, :width] * jnp.repeat(sb, HD, axis=1)
    totals = a[:, width : width + heads] * sa + b[:, width : width + heads] * sb
    pad = a.shape[1] - width - 2 * heads
    return jnp.concatenate([values, totals, top, jnp.zeros((a.shape[0], pad), jnp.float32)], axis=1)


def butterfly_softmax(x, axis, rounds, width, heads):
    size = 1 << sum(len(r) for r in rounds)
    for r in rounds:
        if len(r) == 1:
            x = merge_softmax(x, exchange(x, axis, r[0], size), width, heads)
        else:
            a, b = r
            pa, pb, pc = (exchange(x, axis, m, size) for m in (a, b, a ^ b))
            x = merge_softmax(merge_softmax(x, pa, width, heads), merge_softmax(pb, pc, width, heads), width, heads)
    return x


RINGS = {"seq": {32: (4, 8)}, "tensor": {8: (4, 2)}}


def axis_masks(axis, size):
    rings = RINGS[axis].get(size, (size,))
    return butterfly_rounds(rings)


def shards(
    features,
    input_norm_scale,
    query_key_value_weight,
    adapter_down_weight,
    adapter_up_weight,
    output_weight,
    cached_key_rows,
    cached_value_rows,
    lengths,
    sinks,
    windows,
    seq_masks,
    tensor_masks,
):
    rows = features.shape[0]
    count, span = cached_key_rows.shape[0], cached_key_rows.shape[1]
    local = adapter_up_weight.shape[1]
    heads = local // HD
    rank = adapter_down_weight.shape[1]
    f32, bf16 = jnp.float32, jnp.bfloat16

    feat = features.astype(f32)
    scaled = (feat * input_norm_scale).astype(bf16)

    def project(j):
        return jnp.dot(scaled, query_key_value_weight[:, j, :], preferred_element_type=f32)

    partial_low = jnp.dot(scaled, adapter_down_weight, preferred_element_type=f32)
    partial_sq = jnp.sum(feat * feat, axis=1, keepdims=True)
    packed = jnp.concatenate(
        [project(0), partial_low, partial_sq, jnp.zeros((rows, 127), f32)], axis=1
    )
    summed = butterfly_sum(packed, "seq", seq_masks)
    kv_partial, summed = lax.optimization_barrier(
        (jnp.concatenate([project(1), project(2)], axis=1), summed)
    )
    kv_summed = butterfly_sum(kv_partial, "seq", [(m,) for r in seq_masks for m in r])
    low = summed[:, local : local + rank]
    total_sq = summed[:, local + rank]
    scale_rows = lax.rsqrt(total_sq / INPUT_WIDTH + 1e-05)[:, None]
    lowrank = (low * scale_rows).astype(bf16)
    query_adapter = jnp.dot(lowrank, adapter_up_weight, preferred_element_type=f32)
    queries = (summed[:, :local] * scale_rows + query_adapter).astype(bf16)
    keys_full = kv_summed[:, :local] * scale_rows
    values_full = kv_summed[:, local:] * scale_rows
    new_keys = keys_full.astype(bf16)
    new_values = values_full.astype(bf16)

    col_head = jnp.arange(local, dtype=jnp.int32) // HD
    head_mask = col_head[None, :] == jnp.arange(heads, dtype=jnp.int32)[:, None]
    q_rows = queries.reshape(count, NEW, local)
    q_block = jnp.where(head_mask[None, :, None, :], q_rows[:, None, :, :], jnp.zeros((), bf16))
    q_block = q_block.reshape(count, heads * NEW, local)
    raw = jnp.einsum(
        "rnc,rpc->rnp", q_block, cached_key_rows, preferred_element_type=f32
    ) * HD ** (-0.5)
    base = lax.axis_index("seq") * span
    position = base + jnp.arange(span, dtype=jnp.int32)
    order = jnp.arange(NEW, dtype=jnp.int32)
    length = lengths[:, None, None]
    sink = sinks[:, None, None]
    window = windows[:, None, None]
    pos = position[None, None, :]
    seen = (pos < length) & ((pos < sink) | (length + order[None, :, None] - pos < window))
    seen = jnp.broadcast_to(seen[:, None], (count, heads, NEW, span)).reshape(count, heads * NEW, span)
    scores = jnp.where(seen, raw, NEG)
    local_top = jnp.max(scores, axis=-1)
    expo = jnp.where(scores > CUT, jnp.exp(scores - local_top[..., None]), 0.0)
    local_total = jnp.sum(expo, axis=-1)
    weighted = jnp.einsum(
        "rnp,rpc->rnc", expo.astype(bf16), cached_value_rows, preferred_element_type=f32
    )
    weighted = jnp.sum(
        jnp.where(head_mask[None, :, None, :], weighted.reshape(count, heads, NEW, local), 0.0),
        axis=1,
    )

    def by_row(x):
        return x.reshape(count, heads, NEW).transpose(0, 2, 1).reshape(rows, heads)

    packed = jnp.concatenate(
        [
            weighted.reshape(rows, local),
            by_row(local_total),
            by_row(local_top),
            jnp.zeros((rows, 128 - 2 * heads), f32),
        ],
        axis=1,
    )
    merged = butterfly_softmax(packed, "seq", seq_masks, local, heads)
    cache_out = merged[:, :local]
    cache_total = merged[:, local : local + heads]
    cache_top = merged[:, local + heads : local + 2 * heads]

    query_all = queries.reshape(count, NEW, heads, HD)
    key_all = new_keys.reshape(count, NEW, heads, HD)
    value_all = new_values.reshape(count, NEW, heads, HD)
    fresh = jnp.einsum(
        "rthd,ruhd->rhtu", query_all, key_all, preferred_element_type=f32
    ) * HD ** (-0.5)
    causal = order[:, None] >= order[None, :]
    fresh = jnp.where(causal[None, None], fresh, NEG)
    own_top = by_row(jnp.max(fresh, axis=-1))
    top = jnp.maximum(cache_top, own_top)
    top_rht = top.reshape(count, NEW, heads).transpose(0, 2, 1)
    own_e = jnp.where(fresh > CUT, jnp.exp(fresh - top_rht[..., None]), 0.0)
    own_total = by_row(jnp.sum(own_e, axis=-1))
    own_out = jnp.einsum(
        "rhtu,ruhd->rthd", own_e.astype(bf16), value_all, preferred_element_type=f32
    ).reshape(rows, local)
    cache_scale = jnp.exp(cache_top - top)
    output = cache_out * jnp.repeat(cache_scale, HD, axis=1) + own_out
    total = cache_total * cache_scale + own_total
    attn = (output / jnp.repeat(total, HD, axis=1)).astype(bf16)
    partial_out = jnp.dot(attn, output_weight, preferred_element_type=f32)
    mixed = butterfly_sum(partial_out, "tensor", tensor_masks)
    return (mixed, jnp.stack([keys_full, values_full]))


def solution(mesh):
    in_specs = (
        P(None, "seq"),
        P("seq"),
        P("seq", None, "tensor"),
        P("seq", None),
        P(None, "tensor"),
        P("tensor", "seq"),
        P(None, "seq", "tensor"),
        P(None, "seq", "tensor"),
        P(),
        P(),
        P(),
    )
    out_specs = (P(None, "seq"), P(None, None, "tensor"))
    seq_masks = axis_masks("seq", mesh.shape["seq"])
    tensor_masks = axis_masks("tensor", mesh.shape["tensor"])

    def body(*args):
        return shards(*args, seq_masks, tensor_masks)

    return jax.shard_map(body, mesh=mesh, in_specs=in_specs, out_specs=out_specs, check_vma=False)
```

```python
import jax
import jax.numpy as jnp
from jax import lax
from jax.sharding import PartitionSpec as P

HD = 224
NEW = 4
INPUT_WIDTH = 7168


NEG = -1e30
CUT = -1e29


def butterfly_rounds(axes):
    rounds, shift = [], 0
    for size in reversed(axes):
        masks, bit = [], 1
        while bit < size:
            masks.append((bit if 2 * bit < size or size <= 2 else size - 2 if size > 4 else size - 1) << shift)
            bit *= 2
        rounds += [tuple(masks[i : i + 2]) for i in range(0, len(masks), 2)]
        shift += size.bit_length() - 1
    return rounds


def exchange(x, axis, mask, size):
    return lax.ppermute(x, axis, [(i, i ^ mask) for i in range(size)])


def butterfly_sum(x, axis, rounds):
    size = 1 << sum(len(r) for r in rounds)
    for r in rounds:
        if len(r) == 1:
            x = x + exchange(x, axis, r[0], size)
        else:
            a, b = r
            pa, pb, pc = (exchange(x, axis, m, size) for m in (a, b, a ^ b))
            x = (x + pa) + (pb + pc)
    return x


def merge_softmax(a, b, width, heads, extra):
    n = a.shape[1] - extra
    top = jnp.maximum(a[:, width + heads : width + 2 * heads], b[:, width + heads : width + 2 * heads])
    sa = jnp.exp(a[:, width + heads : width + 2 * heads] - top)
    sb = jnp.exp(b[:, width + heads : width + 2 * heads] - top)
    values = a[:, :width] * jnp.repeat(sa, HD, axis=1) + b[:, :width] * jnp.repeat(sb, HD, axis=1)
    totals = a[:, width : width + heads] * sa + b[:, width : width + heads] * sb
    pad = n - width - 2 * heads
    return jnp.concatenate(
        [values, totals, top, jnp.zeros((a.shape[0], pad), jnp.float32), a[:, n:] + b[:, n:]], axis=1
    )


def butterfly_softmax(x, axis, rounds, width, heads, extra):
    size = 1 << sum(len(r) for r in rounds)
    for r in rounds:
        if len(r) == 1:
            x = merge_softmax(x, exchange(x, axis, r[0], size), width, heads, extra)
        else:
            a, b = r
            pa, pb, pc = (exchange(x, axis, m, size) for m in (a, b, a ^ b))
            x = merge_softmax(
                merge_softmax(x, pa, width, heads, extra), merge_softmax(pb, pc, width, heads, extra),
                width, heads, extra,
            )
    return x


RINGS = {"seq": {32: (4, 8)}, "tensor": {8: (4, 2)}}


def axis_masks(axis, size):
    rings = RINGS[axis].get(size, (size,))
    return butterfly_rounds(rings)


def shards(
    features,
    input_norm_scale,
    query_key_value_weight,
    adapter_down_weight,
    adapter_up_weight,
    output_weight,
    cached_key_rows,
    cached_value_rows,
    lengths,
    sinks,
    windows,
    seq_masks,
    tensor_masks,
):
    rows = features.shape[0]
    count, span = cached_key_rows.shape[0], cached_key_rows.shape[1]
    local = adapter_up_weight.shape[1]
    heads = local // HD
    rank = adapter_down_weight.shape[1]
    f32, bf16 = jnp.float32, jnp.bfloat16

    feat = features.astype(f32)
    scaled = (feat * input_norm_scale).astype(bf16)

    def project(j):
        return jnp.dot(scaled, query_key_value_weight[:, j, :], preferred_element_type=f32)

    partial_low = jnp.dot(scaled, adapter_down_weight, preferred_element_type=f32)
    partial_sq = jnp.sum(feat * feat, axis=1, keepdims=True)
    packed = jnp.concatenate(
        [project(0), partial_low, partial_sq, jnp.zeros((rows, 127), f32)], axis=1
    )
    summed = butterfly_sum(packed, "seq", seq_masks)
    kv_partial = jnp.concatenate([project(1), project(2)], axis=1)
    low = summed[:, local : local + rank]
    total_sq = summed[:, local + rank]
    scale_rows = lax.rsqrt(total_sq / INPUT_WIDTH + 1e-05)[:, None]
    lowrank = (low * scale_rows).astype(bf16)
    query_adapter = jnp.dot(lowrank, adapter_up_weight, preferred_element_type=f32)
    queries = (summed[:, :local] * scale_rows + query_adapter).astype(bf16)

    col_head = jnp.arange(local, dtype=jnp.int32) // HD
    head_mask = col_head[None, :] == jnp.arange(heads, dtype=jnp.int32)[:, None]
    q_rows = queries.reshape(count, NEW, local)
    q_block = jnp.where(head_mask[None, :, None, :], q_rows[:, None, :, :], jnp.zeros((), bf16))
    q_block = q_block.reshape(count, heads * NEW, local)
    raw = jnp.einsum(
        "rnc,rpc->rnp", q_block, cached_key_rows, preferred_element_type=f32
    ) * HD ** (-0.5)
    base = lax.axis_index("seq") * span
    position = base + jnp.arange(span, dtype=jnp.int32)
    order = jnp.arange(NEW, dtype=jnp.int32)
    length = lengths[:, None, None]
    sink = sinks[:, None, None]
    window = windows[:, None, None]
    pos = position[None, None, :]
    seen = (pos < length) & ((pos < sink) | (length + order[None, :, None] - pos < window))
    seen = jnp.broadcast_to(seen[:, None], (count, heads, NEW, span)).reshape(count, heads * NEW, span)
    scores = jnp.where(seen, raw, NEG)
    local_top = jnp.max(scores, axis=-1)
    expo = jnp.where(scores > CUT, jnp.exp(scores - local_top[..., None]), 0.0)
    local_total = jnp.sum(expo, axis=-1)
    weighted = jnp.einsum(
        "rnp,rpc->rnc", expo.astype(bf16), cached_value_rows, preferred_element_type=f32
    )
    weighted = jnp.sum(
        jnp.where(head_mask[None, :, None, :], weighted.reshape(count, heads, NEW, local), 0.0),
        axis=1,
    )

    def by_row(x):
        return x.reshape(count, heads, NEW).transpose(0, 2, 1).reshape(rows, heads)

    packed = jnp.concatenate(
        [
            weighted.reshape(rows, local),
            by_row(local_total),
            by_row(local_top),
            jnp.zeros((rows, 128 - 2 * heads), f32),
            kv_partial,
        ],
        axis=1,
    )
    merged = butterfly_softmax(packed, "seq", seq_masks, local, heads, kv_partial.shape[1])
    kv_summed = merged[:, local + 128 :]
    keys_full = kv_summed[:, :local] * scale_rows
    values_full = kv_summed[:, local:] * scale_rows
    new_keys = keys_full.astype(bf16)
    new_values = values_full.astype(bf16)
    cache_out = merged[:, :local]
    cache_total = merged[:, local : local + heads]
    cache_top = merged[:, local + heads : local + 2 * heads]

    query_all = queries.reshape(count, NEW, heads, HD)
    key_all = new_keys.reshape(count, NEW, heads, HD)
    value_all = new_values.reshape(count, NEW, heads, HD)
    fresh = jnp.einsum(
        "rthd,ruhd->rhtu", query_all, key_all, preferred_element_type=f32
    ) * HD ** (-0.5)
    causal = order[:, None] >= order[None, :]
    fresh = jnp.where(causal[None, None], fresh, NEG)
    own_top = by_row(jnp.max(fresh, axis=-1))
    top = jnp.maximum(cache_top, own_top)
    top_rht = top.reshape(count, NEW, heads).transpose(0, 2, 1)
    own_e = jnp.where(fresh > CUT, jnp.exp(fresh - top_rht[..., None]), 0.0)
    own_total = by_row(jnp.sum(own_e, axis=-1))
    own_out = jnp.einsum(
        "rhtu,ruhd->rthd", own_e.astype(bf16), value_all, preferred_element_type=f32
    ).reshape(rows, local)
    cache_scale = jnp.exp(cache_top - top)
    output = cache_out * jnp.repeat(cache_scale, HD, axis=1) + own_out
    total = cache_total * cache_scale + own_total
    attn = (output / jnp.repeat(total, HD, axis=1)).astype(bf16)
    partial_out = jnp.dot(attn, output_weight, preferred_element_type=f32)
    mixed = butterfly_sum(partial_out, "tensor", tensor_masks)
    return (mixed, jnp.stack([keys_full, values_full]))


def solution(mesh):
    in_specs = (
        P(None, "seq"),
        P("seq"),
        P("seq", None, "tensor"),
        P("seq", None),
        P(None, "tensor"),
        P("tensor", "seq"),
        P(None, "seq", "tensor"),
        P(None, "seq", "tensor"),
        P(),
        P(),
        P(),
    )
    out_specs = (P(None, "seq"), P(None, None, "tensor"))
    seq_masks = axis_masks("seq", mesh.shape["seq"])
    tensor_masks = axis_masks("tensor", mesh.shape["tensor"])

    def body(*args):
        return shards(*args, seq_masks, tensor_masks)

    return jax.shard_map(body, mesh=mesh, in_specs=in_specs, out_specs=out_specs, check_vma=False)
```

```python
import jax
import jax.numpy as jnp
from jax import lax
from jax.sharding import PartitionSpec as P

HD = 224
NEW = 4
INPUT_WIDTH = 7168


NEG = -1e30
CUT = -1e29


def butterfly_rounds(axes):
    rounds, shift = [], 0
    for size in reversed(axes):
        masks, bit = [], 1
        while bit < size:
            masks.append((bit if 2 * bit < size or size <= 2 else size - 2 if size > 4 else size - 1) << shift)
            bit *= 2
        rounds += [tuple(masks[i : i + 2]) for i in range(0, len(masks), 2)]
        shift += size.bit_length() - 1
    return rounds


def exchange(x, axis, mask, size):
    return lax.ppermute(x, axis, [(i, i ^ mask) for i in range(size)])


def butterfly_sum(x, axis, rounds):
    size = 1 << sum(len(r) for r in rounds)
    for r in rounds:
        if len(r) == 1:
            x = x + exchange(x, axis, r[0], size)
        else:
            a, b = r
            pa, pb, pc = (exchange(x, axis, m, size) for m in (a, b, a ^ b))
            x = (x + pa) + (pb + pc)
    return x


def merge_softmax(a, b, width, heads):
    top = jnp.maximum(a[:, width + heads : width + 2 * heads], b[:, width + heads : width + 2 * heads])
    sa = jnp.exp(a[:, width + heads : width + 2 * heads] - top)
    sb = jnp.exp(b[:, width + heads : width + 2 * heads] - top)
    values = a[:, :width] * jnp.repeat(sa, HD, axis=1) + b[:, :width] * jnp.repeat(sb, HD, axis=1)
    totals = a[:, width : width + heads] * sa + b[:, width : width + heads] * sb
    pad = a.shape[1] - width - 2 * heads
    return jnp.concatenate([values, totals, top, jnp.zeros((a.shape[0], pad), jnp.float32)], axis=1)


def butterfly_softmax(x, axis, rounds, width, heads):
    size = 1 << sum(len(r) for r in rounds)
    for r in rounds:
        if len(r) == 1:
            x = merge_softmax(x, exchange(x, axis, r[0], size), width, heads)
        else:
            a, b = r
            pa, pb, pc = (exchange(x, axis, m, size) for m in (a, b, a ^ b))
            x = merge_softmax(merge_softmax(x, pa, width, heads), merge_softmax(pb, pc, width, heads), width, heads)
    return x


RINGS = {"seq": {32: (4, 8)}, "tensor": {8: (4, 2)}}


def axis_masks(axis, size):
    rings = RINGS[axis].get(size, (size,))
    return sorted(butterfly_rounds(rings), key=len)


def shards(
    features,
    input_norm_scale,
    query_key_value_weight,
    adapter_down_weight,
    adapter_up_weight,
    output_weight,
    cached_key_rows,
    cached_value_rows,
    lengths,
    sinks,
    windows,
    seq_masks,
    tensor_masks,
):
    rows = features.shape[0]
    count, span = cached_key_rows.shape[0], cached_key_rows.shape[1]
    local = adapter_up_weight.shape[1]
    heads = local // HD
    rank = adapter_down_weight.shape[1]
    f32, bf16 = jnp.float32, jnp.bfloat16

    feat = features.astype(f32)
    scaled = (feat * input_norm_scale).astype(bf16)

    def project(j):
        return jnp.dot(scaled, query_key_value_weight[:, j, :], preferred_element_type=f32)

    partial_low = jnp.dot(scaled, adapter_down_weight, preferred_element_type=f32)
    partial_sq = jnp.sum(feat * feat, axis=1, keepdims=True)
    packed = jnp.concatenate(
        [project(0), partial_low, partial_sq, jnp.zeros((rows, 127), f32)], axis=1
    )
    summed = butterfly_sum(packed, "seq", seq_masks)
    kv_summed = butterfly_sum(jnp.concatenate([project(1), project(2)], axis=1), "seq", seq_masks)
    low = summed[:, local : local + rank]
    total_sq = summed[:, local + rank]
    scale_rows = lax.rsqrt(total_sq / INPUT_WIDTH + 1e-05)[:, None]
    lowrank = (low * scale_rows).astype(bf16)
    query_adapter = jnp.dot(lowrank, adapter_up_weight, preferred_element_type=f32)
    queries = (summed[:, :local] * scale_rows + query_adapter).astype(bf16)
    keys_full = kv_summed[:, :local] * scale_rows
    values_full = kv_summed[:, local:] * scale_rows
    new_keys = keys_full.astype(bf16)
    new_values = values_full.astype(bf16)

    col_head = jnp.arange(local, dtype=jnp.int32) // HD
    head_mask = col_head[None, :] == jnp.arange(heads, dtype=jnp.int32)[:, None]
    q_rows = queries.reshape(count, NEW, local)
    q_block = jnp.where(head_mask[None, :, None, :], q_rows[:, None, :, :], jnp.zeros((), bf16))
    q_block = q_block.reshape(count, heads * NEW, local)
    raw = jnp.einsum(
        "rnc,rpc->rnp", q_block, cached_key_rows, preferred_element_type=f32
    ) * HD ** (-0.5)
    base = lax.axis_index("seq") * span
    position = base + jnp.arange(span, dtype=jnp.int32)
    order = jnp.arange(NEW, dtype=jnp.int32)
    length = lengths[:, None, None]
    sink = sinks[:, None, None]
    window = windows[:, None, None]
    pos = position[None, None, :]
    seen = (pos < length) & ((pos < sink) | (length + order[None, :, None] - pos < window))
    seen = jnp.broadcast_to(seen[:, None], (count, heads, NEW, span)).reshape(count, heads * NEW, span)
    scores = jnp.where(seen, raw, NEG)
    local_top = jnp.max(scores, axis=-1)
    expo = jnp.where(scores > CUT, jnp.exp(scores - local_top[..., None]), 0.0)
    local_total = jnp.sum(expo, axis=-1)
    weighted = jnp.einsum(
        "rnp,rpc->rnc", expo.astype(bf16), cached_value_rows, preferred_element_type=f32
    )
    weighted = jnp.sum(
        jnp.where(head_mask[None, :, None, :], weighted.reshape(count, heads, NEW, local), 0.0),
        axis=1,
    )

    def by_row(x):
        return x.reshape(count, heads, NEW).transpose(0, 2, 1).reshape(rows, heads)

    packed = jnp.concatenate(
        [
            weighted.reshape(rows, local),
            by_row(local_total),
            by_row(local_top),
            jnp.zeros((rows, 128 - 2 * heads), f32),
        ],
        axis=1,
    )
    merged = butterfly_softmax(packed, "seq", seq_masks, local, heads)
    cache_out = merged[:, :local]
    cache_total = merged[:, local : local + heads]
    cache_top = merged[:, local + heads : local + 2 * heads]

    query_all = queries.reshape(count, NEW, heads, HD)
    key_all = new_keys.reshape(count, NEW, heads, HD)
    value_all = new_values.reshape(count, NEW, heads, HD)
    fresh = jnp.einsum(
        "rthd,ruhd->rhtu", query_all, key_all, preferred_element_type=f32
    ) * HD ** (-0.5)
    causal = order[:, None] >= order[None, :]
    fresh = jnp.where(causal[None, None], fresh, NEG)
    own_top = by_row(jnp.max(fresh, axis=-1))
    top = jnp.maximum(cache_top, own_top)
    top_rht = top.reshape(count, NEW, heads).transpose(0, 2, 1)
    own_e = jnp.where(fresh > CUT, jnp.exp(fresh - top_rht[..., None]), 0.0)
    own_total = by_row(jnp.sum(own_e, axis=-1))
    own_out = jnp.einsum(
        "rhtu,ruhd->rthd", own_e.astype(bf16), value_all, preferred_element_type=f32
    ).reshape(rows, local)
    cache_scale = jnp.exp(cache_top - top)
    output = cache_out * jnp.repeat(cache_scale, HD, axis=1) + own_out
    total = cache_total * cache_scale + own_total
    attn = (output / jnp.repeat(total, HD, axis=1)).astype(bf16)
    partial_out = jnp.dot(attn, output_weight, preferred_element_type=f32)
    mixed = butterfly_sum(partial_out, "tensor", tensor_masks)
    return (mixed, jnp.stack([keys_full, values_full]))


def solution(mesh):
    in_specs = (
        P(None, "seq"),
        P("seq"),
        P("seq", None, "tensor"),
        P("seq", None),
        P(None, "tensor"),
        P("tensor", "seq"),
        P(None, "seq", "tensor"),
        P(None, "seq", "tensor"),
        P(),
        P(),
        P(),
    )
    out_specs = (P(None, "seq"), P(None, None, "tensor"))
    seq_masks = axis_masks("seq", mesh.shape["seq"])
    tensor_masks = axis_masks("tensor", mesh.shape["tensor"])

    def body(*args):
        return shards(*args, seq_masks, tensor_masks)

    return jax.shard_map(body, mesh=mesh, in_specs=in_specs, out_specs=out_specs, check_vma=False)
```

```python
import jax
import jax.numpy as jnp
from jax import lax
from jax.sharding import PartitionSpec as P

HD = 224
NEW = 4
INPUT_WIDTH = 7168


NEG = -1e30
CUT = -1e29


def butterfly_rounds(axes):
    rounds, shift = [], 0
    for size in reversed(axes):
        masks, bit = [], 1
        while bit < size:
            masks.append((bit if 2 * bit < size or size <= 2 else size - 2 if size > 4 else size - 1) << shift)
            bit *= 2
        rounds += [tuple(masks[i : i + 2]) for i in range(0, len(masks), 2)]
        shift += size.bit_length() - 1
    return rounds


def exchange(x, axis, mask, size):
    return lax.ppermute(x, axis, [(i, i ^ mask) for i in range(size)])


def butterfly_sum(x, axis, rounds):
    size = 1 << sum(len(r) for r in rounds)
    for r in rounds:
        if len(r) == 1:
            x = x + exchange(x, axis, r[0], size)
        else:
            a, b = r
            pa, pb, pc = (exchange(x, axis, m, size) for m in (a, b, a ^ b))
            x = (x + pa) + (pb + pc)
    return x


def merge_softmax(a, b, width, heads):
    top = jnp.maximum(a[:, width + heads : width + 2 * heads], b[:, width + heads : width + 2 * heads])
    sa = jnp.exp(a[:, width + heads : width + 2 * heads] - top)
    sb = jnp.exp(b[:, width + heads : width + 2 * heads] - top)
    values = a[:, :width] * jnp.repeat(sa, HD, axis=1) + b[:, :width] * jnp.repeat(sb, HD, axis=1)
    totals = a[:, width : width + heads] * sa + b[:, width : width + heads] * sb
    pad = a.shape[1] - width - 2 * heads
    return jnp.concatenate([values, totals, top, jnp.zeros((a.shape[0], pad), jnp.float32)], axis=1)


def butterfly_softmax(x, axis, rounds, width, heads):
    size = 1 << sum(len(r) for r in rounds)
    for r in rounds:
        if len(r) == 1:
            x = merge_softmax(x, exchange(x, axis, r[0], size), width, heads)
        else:
            a, b = r
            pa, pb, pc = (exchange(x, axis, m, size) for m in (a, b, a ^ b))
            x = merge_softmax(merge_softmax(x, pa, width, heads), merge_softmax(pb, pc, width, heads), width, heads)
    return x


RINGS = {"seq": {32: (4, 8)}, "tensor": {8: (4, 2)}}


def axis_masks(axis, size):
    rings = RINGS[axis].get(size, (size,))
    return sorted(butterfly_rounds(rings), key=len)


def shards(
    features,
    input_norm_scale,
    query_key_value_weight,
    adapter_down_weight,
    adapter_up_weight,
    output_weight,
    cached_key_rows,
    cached_value_rows,
    lengths,
    sinks,
    windows,
    seq_masks,
    tensor_masks,
):
    rows = features.shape[0]
    count, span = cached_key_rows.shape[0], cached_key_rows.shape[1]
    local = adapter_up_weight.shape[1]
    heads = local // HD
    rank = adapter_down_weight.shape[1]
    f32, bf16 = jnp.float32, jnp.bfloat16

    feat = features.astype(f32)
    scaled = (feat * input_norm_scale).astype(bf16)

    def project(j):
        return jnp.dot(scaled, query_key_value_weight[:, j, :], preferred_element_type=f32)

    partial_low = jnp.dot(scaled, adapter_down_weight, preferred_element_type=f32)
    partial_sq = jnp.sum(feat * feat, axis=1, keepdims=True)
    packed = jnp.concatenate(
        [project(0), partial_low, partial_sq, jnp.zeros((rows, 127), f32)], axis=1
    )
    summed = butterfly_sum(packed, "seq", seq_masks)
    kv_summed = butterfly_sum(
        jnp.concatenate([project(1), project(2)], axis=1), "seq", [(m,) for r in seq_masks for m in r]
    )
    low = summed[:, local : local + rank]
    total_sq = summed[:, local + rank]
    scale_rows = lax.rsqrt(total_sq / INPUT_WIDTH + 1e-05)[:, None]
    lowrank = (low * scale_rows).astype(bf16)
    query_adapter = jnp.dot(lowrank, adapter_up_weight, preferred_element_type=f32)
    queries = (summed[:, :local] * scale_rows + query_adapter).astype(bf16)
    keys_full = kv_summed[:, :local] * scale_rows
    values_full = kv_summed[:, local:] * scale_rows
    new_keys = keys_full.astype(bf16)
    new_values = values_full.astype(bf16)

    col_head = jnp.arange(local, dtype=jnp.int32) // HD
    head_mask = col_head[None, :] == jnp.arange(heads, dtype=jnp.int32)[:, None]
    q_rows = queries.reshape(count, NEW, local)
    q_block = jnp.where(head_mask[None, :, None, :], q_rows[:, None, :, :], jnp.zeros((), bf16))
    q_block = q_block.reshape(count, heads * NEW, local)
    raw = jnp.einsum(
        "rnc,rpc->rnp", q_block, cached_key_rows, preferred_element_type=f32
    ) * HD ** (-0.5)
    base = lax.axis_index("seq") * span
    position = base + jnp.arange(span, dtype=jnp.int32)
    order = jnp.arange(NEW, dtype=jnp.int32)
    length = lengths[:, None, None]
    sink = sinks[:, None, None]
    window = windows[:, None, None]
    pos = position[None, None, :]
    seen = (pos < length) & ((pos < sink) | (length + order[None, :, None] - pos < window))
    seen = jnp.broadcast_to(seen[:, None], (count, heads, NEW, span)).reshape(count, heads * NEW, span)
    scores = jnp.where(seen, raw, NEG)
    local_top = jnp.max(scores, axis=-1)
    expo = jnp.where(scores > CUT, jnp.exp(scores - local_top[..., None]), 0.0)
    local_total = jnp.sum(expo, axis=-1)
    weighted = jnp.einsum(
        "rnp,rpc->rnc", expo.astype(bf16), cached_value_rows, preferred_element_type=f32
    )
    weighted = jnp.sum(
        jnp.where(head_mask[None, :, None, :], weighted.reshape(count, heads, NEW, local), 0.0),
        axis=1,
    )

    def by_row(x):
        return x.reshape(count, heads, NEW).transpose(0, 2, 1).reshape(rows, heads)

    packed = jnp.concatenate(
        [
            weighted.reshape(rows, local),
            by_row(local_total),
            by_row(local_top),
            jnp.zeros((rows, 128 - 2 * heads), f32),
        ],
        axis=1,
    )
    merged = butterfly_softmax(packed, "seq", seq_masks, local, heads)
    cache_out = merged[:, :local]
    cache_total = merged[:, local : local + heads]
    cache_top = merged[:, local + heads : local + 2 * heads]

    query_all = queries.reshape(count, NEW, heads, HD)
    key_all = new_keys.reshape(count, NEW, heads, HD)
    value_all = new_values.reshape(count, NEW, heads, HD)
    fresh = jnp.einsum(
        "rthd,ruhd->rhtu", query_all, key_all, preferred_element_type=f32
    ) * HD ** (-0.5)
    causal = order[:, None] >= order[None, :]
    fresh = jnp.where(causal[None, None], fresh, NEG)
    own_top = by_row(jnp.max(fresh, axis=-1))
    top = jnp.maximum(cache_top, own_top)
    top_rht = top.reshape(count, NEW, heads).transpose(0, 2, 1)
    own_e = jnp.where(fresh > CUT, jnp.exp(fresh - top_rht[..., None]), 0.0)
    own_total = by_row(jnp.sum(own_e, axis=-1))
    own_out = jnp.einsum(
        "rhtu,ruhd->rthd", own_e.astype(bf16), value_all, preferred_element_type=f32
    ).reshape(rows, local)
    cache_scale = jnp.exp(cache_top - top)
    output = cache_out * jnp.repeat(cache_scale, HD, axis=1) + own_out
    total = cache_total * cache_scale + own_total
    attn = (output / jnp.repeat(total, HD, axis=1)).astype(bf16)
    partial_out = jnp.dot(attn, output_weight, preferred_element_type=f32)
    mixed = butterfly_sum(partial_out, "tensor", tensor_masks)
    return (mixed, jnp.stack([keys_full, values_full]))


def solution(mesh):
    in_specs = (
        P(None, "seq"),
        P("seq"),
        P("seq", None, "tensor"),
        P("seq", None),
        P(None, "tensor"),
        P("tensor", "seq"),
        P(None, "seq", "tensor"),
        P(None, "seq", "tensor"),
        P(),
        P(),
        P(),
    )
    out_specs = (P(None, "seq"), P(None, None, "tensor"))
    seq_masks = axis_masks("seq", mesh.shape["seq"])
    tensor_masks = axis_masks("tensor", mesh.shape["tensor"])

    def body(*args):
        return shards(*args, seq_masks, tensor_masks)

    return jax.shard_map(body, mesh=mesh, in_specs=in_specs, out_specs=out_specs, check_vma=False)
```

```python
import jax
import jax.numpy as jnp
from jax import lax
from jax.sharding import PartitionSpec as P

HD = 224
NEW = 4
INPUT_WIDTH = 7168


NEG = -1e30
CUT = -1e29


def butterfly_rounds(axes):
    rounds, shift = [], 0
    for size in reversed(axes):
        masks, bit = [], 1
        while bit < size:
            masks.append((bit if 2 * bit < size or size <= 2 else size - 2 if size > 4 else size - 1) << shift)
            bit *= 2
        rounds += [tuple(masks[i : i + 2]) for i in range(0, len(masks), 2)]
        shift += size.bit_length() - 1
    return rounds


def exchange(x, axis, mask, size):
    return lax.ppermute(x, axis, [(i, i ^ mask) for i in range(size)])


def butterfly_sum(x, axis, rounds):
    size = 1 << sum(len(r) for r in rounds)
    for r in rounds:
        if len(r) == 1:
            x = x + exchange(x, axis, r[0], size)
        else:
            a, b = r
            pa, pb, pc = (exchange(x, axis, m, size) for m in (a, b, a ^ b))
            x = (x + pa) + (pb + pc)
    return x


def merge_softmax(a, b, width, heads):
    top = jnp.maximum(a[:, width + heads : width + 2 * heads], b[:, width + heads : width + 2 * heads])
    sa = jnp.exp(a[:, width + heads : width + 2 * heads] - top)
    sb = jnp.exp(b[:, width + heads : width + 2 * heads] - top)
    values = a[:, :width] * jnp.repeat(sa, HD, axis=1) + b[:, :width] * jnp.repeat(sb, HD, axis=1)
    totals = a[:, width : width + heads] * sa + b[:, width : width + heads] * sb
    pad = a.shape[1] - width - 2 * heads
    return jnp.concatenate([values, totals, top, jnp.zeros((a.shape[0], pad), jnp.float32)], axis=1)


def butterfly_softmax(x, axis, rounds, width, heads):
    size = 1 << sum(len(r) for r in rounds)
    for r in rounds:
        if len(r) == 1:
            x = merge_softmax(x, exchange(x, axis, r[0], size), width, heads)
        else:
            a, b = r
            pa, pb, pc = (exchange(x, axis, m, size) for m in (a, b, a ^ b))
            x = merge_softmax(merge_softmax(x, pa, width, heads), merge_softmax(pb, pc, width, heads), width, heads)
    return x


RINGS = {"seq": {32: (4, 8)}, "tensor": {8: (4, 2)}}


def axis_masks(axis, size):
    rings = RINGS[axis].get(size, (size,))
    return sorted(butterfly_rounds(rings), key=len)


def shards(
    features,
    input_norm_scale,
    query_key_value_weight,
    adapter_down_weight,
    adapter_up_weight,
    output_weight,
    cached_key_rows,
    cached_value_rows,
    lengths,
    sinks,
    windows,
    seq_masks,
    tensor_masks,
):
    rows = features.shape[0]
    count, span = cached_key_rows.shape[0], cached_key_rows.shape[1]
    local = adapter_up_weight.shape[1]
    heads = local // HD
    rank = adapter_down_weight.shape[1]
    f32, bf16 = jnp.float32, jnp.bfloat16

    feat = features.astype(f32)
    scaled = (feat * input_norm_scale).astype(bf16)

    def project(j):
        return jnp.dot(scaled, query_key_value_weight[:, j, :], preferred_element_type=f32)

    partial_low = jnp.dot(scaled, adapter_down_weight, preferred_element_type=f32)
    partial_sq = jnp.sum(feat * feat, axis=1, keepdims=True)
    packed = jnp.concatenate(
        [project(0), partial_low, partial_sq, jnp.zeros((rows, 127), f32)], axis=1
    )
    summed = butterfly_sum(packed, "seq", seq_masks)
    kv_summed = butterfly_sum(
        jnp.concatenate([project(1), project(2)], axis=1), "seq", [(m,) for r in seq_masks for m in r]
    )
    low = summed[:, local : local + rank]
    total_sq = summed[:, local + rank]
    scale_rows = lax.rsqrt(total_sq / INPUT_WIDTH + 1e-05)[:, None]
    lowrank = (low * scale_rows).astype(bf16)
    query_adapter = jnp.dot(lowrank, adapter_up_weight, preferred_element_type=f32)
    queries = (summed[:, :local] * scale_rows + query_adapter).astype(bf16)
    keys_full = kv_summed[:, :local] * scale_rows
    values_full = kv_summed[:, local:] * scale_rows
    new_keys = keys_full.astype(bf16)
    new_values = values_full.astype(bf16)

    col_head = jnp.arange(local, dtype=jnp.int32) // HD
    head_mask = col_head[None, :] == jnp.arange(heads, dtype=jnp.int32)[:, None]
    q_rows = queries.reshape(count, NEW, local)
    q_block = jnp.where(head_mask[None, :, None, :], q_rows[:, None, :, :], jnp.zeros((), bf16))
    q_block = q_block.reshape(count, heads * NEW, local)
    raw = jnp.einsum(
        "rnc,rpc->rnp", q_block, cached_key_rows, preferred_element_type=f32
    ) * HD ** (-0.5)
    base = lax.axis_index("seq") * span
    position = base + jnp.arange(span, dtype=jnp.int32)
    order = jnp.arange(NEW, dtype=jnp.int32)
    length = lengths[:, None, None]
    sink = sinks[:, None, None]
    window = windows[:, None, None]
    pos = position[None, None, :]
    seen = (pos < length) & ((pos < sink) | (length + order[None, :, None] - pos < window))
    seen = jnp.broadcast_to(seen[:, None], (count, heads, NEW, span)).reshape(count, heads * NEW, span)
    scores = jnp.where(seen, raw, NEG)
    local_top = jnp.max(scores, axis=-1)
    expo = jnp.where(scores > CUT, jnp.exp(scores - local_top[..., None]), 0.0)
    local_total = jnp.sum(expo, axis=-1)
    weighted = jnp.einsum(
        "rnp,rpc->rnc", expo.astype(bf16), cached_value_rows, preferred_element_type=f32
    )
    weighted = jnp.sum(
        jnp.where(head_mask[None, :, None, :], weighted.reshape(count, heads, NEW, local), 0.0),
        axis=1,
    )

    def by_row(x):
        return x.reshape(count, heads, NEW).transpose(0, 2, 1).reshape(rows, heads)

    packed = jnp.concatenate(
        [
            weighted.reshape(rows, local),
            by_row(local_total),
            by_row(local_top),
            jnp.zeros((rows, 128 - 2 * heads), f32),
        ],
        axis=1,
    )
    merged = butterfly_softmax(packed, "seq", seq_masks, local, heads)
    cache_out = merged[:, :local]
    cache_total = merged[:, local : local + heads]
    cache_top = merged[:, local + heads : local + 2 * heads]

    query_all = queries.reshape(count, NEW, heads, HD)
    key_all = new_keys.reshape(count, NEW, heads, HD)
    value_all = new_values.reshape(count, NEW, heads, HD)
    fresh = jnp.einsum(
        "rthd,ruhd->rhtu", query_all, key_all, preferred_element_type=f32
    ) * HD ** (-0.5)
    causal = order[:, None] >= order[None, :]
    fresh = jnp.where(causal[None, None], fresh, NEG)
    own_top_rht = jnp.max(fresh, axis=-1)
    own_e = jnp.where(fresh > CUT, jnp.exp(fresh - own_top_rht[..., None]), 0.0)
    own_total = by_row(jnp.sum(own_e, axis=-1))
    own_out = jnp.einsum(
        "rhtu,ruhd->rthd", own_e.astype(bf16), value_all, preferred_element_type=f32
    ).reshape(rows, local)
    own_top = by_row(own_top_rht)
    top = jnp.maximum(cache_top, own_top)
    cache_scale = jnp.exp(cache_top - top)
    own_scale = jnp.exp(own_top - top)
    output = cache_out * jnp.repeat(cache_scale, HD, axis=1) + own_out * jnp.repeat(own_scale, HD, axis=1)
    total = cache_total * cache_scale + own_total * own_scale
    attn = (output / jnp.repeat(total, HD, axis=1)).astype(bf16)
    partial_out = jnp.dot(attn, output_weight, preferred_element_type=f32)
    mixed = butterfly_sum(partial_out, "tensor", tensor_masks)
    return (mixed, jnp.stack([keys_full, values_full]))


def solution(mesh):
    in_specs = (
        P(None, "seq"),
        P("seq"),
        P("seq", None, "tensor"),
        P("seq", None),
        P(None, "tensor"),
        P("tensor", "seq"),
        P(None, "seq", "tensor"),
        P(None, "seq", "tensor"),
        P(),
        P(),
        P(),
    )
    out_specs = (P(None, "seq"), P(None, None, "tensor"))
    seq_masks = axis_masks("seq", mesh.shape["seq"])
    tensor_masks = axis_masks("tensor", mesh.shape["tensor"])

    def body(*args):
        return shards(*args, seq_masks, tensor_masks)

    return jax.shard_map(body, mesh=mesh, in_specs=in_specs, out_specs=out_specs, check_vma=False)
```

```python
import jax
import jax.numpy as jnp
from jax import lax
from jax.sharding import PartitionSpec as P

HD = 224
NEW = 4
INPUT_WIDTH = 7168


NEG = -1e30
CUT = -1e29


def butterfly_rounds(axes):
    rounds, shift = [], 0
    for size in reversed(axes):
        masks, bit = [], 1
        while bit < size:
            masks.append((bit if 2 * bit < size or size <= 2 else size - 2 if size > 4 else size - 1) << shift)
            bit *= 2
        rounds += [tuple(masks[i : i + 2]) for i in range(0, len(masks), 2)]
        shift += size.bit_length() - 1
    return rounds


def exchange(x, axis, mask, size):
    return lax.ppermute(x, axis, [(i, i ^ mask) for i in range(size)])


def butterfly_sum(x, axis, rounds):
    size = 1 << sum(len(r) for r in rounds)
    for r in rounds:
        if len(r) == 1:
            x = x + exchange(x, axis, r[0], size)
        else:
            a, b = r
            pa, pb, pc = (exchange(x, axis, m, size) for m in (a, b, a ^ b))
            x = (x + pa) + (pb + pc)
    return x


def per_column(s, width):
    col = lax.broadcasted_iota(jnp.int32, (s.shape[0], width), 1) // HD
    out = jnp.broadcast_to(s[:, 0:1], (s.shape[0], width))
    for h in range(1, s.shape[1]):
        out = jnp.where(col == h, s[:, h : h + 1], out)
    return out


def merge_softmax(a, b, width, heads):
    top = jnp.maximum(a[:, width + heads : width + 2 * heads], b[:, width + heads : width + 2 * heads])
    sa = jnp.exp(a[:, width + heads : width + 2 * heads] - top)
    sb = jnp.exp(b[:, width + heads : width + 2 * heads] - top)
    values = a[:, :width] * per_column(sa, width) + b[:, :width] * per_column(sb, width)
    totals = a[:, width : width + heads] * sa + b[:, width : width + heads] * sb
    pad = a.shape[1] - width - 2 * heads
    return jnp.concatenate([values, totals, top, jnp.zeros((a.shape[0], pad), jnp.float32)], axis=1)


def butterfly_softmax(x, axis, rounds, width, heads):
    size = 1 << sum(len(r) for r in rounds)
    for r in rounds:
        if len(r) == 1:
            x = merge_softmax(x, exchange(x, axis, r[0], size), width, heads)
        else:
            a, b = r
            pa, pb, pc = (exchange(x, axis, m, size) for m in (a, b, a ^ b))
            x = merge_softmax(merge_softmax(x, pa, width, heads), merge_softmax(pb, pc, width, heads), width, heads)
    return x


RINGS = {"seq": {32: (4, 8)}, "tensor": {8: (4, 2)}}


def axis_masks(axis, size):
    rings = RINGS[axis].get(size, (size,))
    return sorted(butterfly_rounds(rings), key=len)


def shards(
    features,
    input_norm_scale,
    query_key_value_weight,
    adapter_down_weight,
    adapter_up_weight,
    output_weight,
    cached_key_rows,
    cached_value_rows,
    lengths,
    sinks,
    windows,
    seq_masks,
    tensor_masks,
):
    rows = features.shape[0]
    count, span = cached_key_rows.shape[0], cached_key_rows.shape[1]
    local = adapter_up_weight.shape[1]
    heads = local // HD
    rank = adapter_down_weight.shape[1]
    f32, bf16 = jnp.float32, jnp.bfloat16

    feat = features.astype(f32)
    scaled = (feat * input_norm_scale).astype(bf16)

    def project(j):
        return jnp.dot(scaled, query_key_value_weight[:, j, :], preferred_element_type=f32)

    partial_low = jnp.dot(scaled, adapter_down_weight, preferred_element_type=f32)
    partial_sq = jnp.sum(feat * feat, axis=1, keepdims=True)
    packed = jnp.concatenate(
        [project(0), partial_low, partial_sq, jnp.zeros((rows, 127), f32)], axis=1
    )
    summed = butterfly_sum(packed, "seq", seq_masks)
    kv_summed = butterfly_sum(
        jnp.concatenate([project(1), project(2)], axis=1), "seq", [(m,) for r in seq_masks for m in r]
    )
    low = summed[:, local : local + rank]
    total_sq = summed[:, local + rank]
    scale_rows = lax.rsqrt(total_sq / INPUT_WIDTH + 1e-05)[:, None]
    lowrank = (low * scale_rows).astype(bf16)
    query_adapter = jnp.dot(lowrank, adapter_up_weight, preferred_element_type=f32)
    queries = (summed[:, :local] * scale_rows + query_adapter).astype(bf16)
    keys_full = kv_summed[:, :local] * scale_rows
    values_full = kv_summed[:, local:] * scale_rows
    new_keys = keys_full.astype(bf16)
    new_values = values_full.astype(bf16)

    col_head = jnp.arange(local, dtype=jnp.int32) // HD
    head_mask = col_head[None, :] == jnp.arange(heads, dtype=jnp.int32)[:, None]
    q_rows = queries.reshape(count, NEW, local)
    q_block = jnp.where(head_mask[None, :, None, :], q_rows[:, None, :, :], jnp.zeros((), bf16))
    q_block = q_block.reshape(count, heads * NEW, local)
    raw = jnp.einsum(
        "rnc,rpc->rnp", q_block, cached_key_rows, preferred_element_type=f32
    ) * HD ** (-0.5)
    base = lax.axis_index("seq") * span
    position = base + jnp.arange(span, dtype=jnp.int32)
    order = jnp.arange(NEW, dtype=jnp.int32)
    length = lengths[:, None, None]
    sink = sinks[:, None, None]
    window = windows[:, None, None]
    pos = position[None, None, :]
    seen = (pos < length) & ((pos < sink) | (length + order[None, :, None] - pos < window))
    seen = jnp.broadcast_to(seen[:, None], (count, heads, NEW, span)).reshape(count, heads * NEW, span)
    scores = jnp.where(seen, raw, NEG)
    local_top = jnp.max(scores, axis=-1)
    expo = jnp.where(scores > CUT, jnp.exp(scores - local_top[..., None]), 0.0)
    local_total = jnp.sum(expo, axis=-1)
    weighted = jnp.einsum(
        "rnp,rpc->rnc", expo.astype(bf16), cached_value_rows, preferred_element_type=f32
    )
    weighted = jnp.sum(
        jnp.where(head_mask[None, :, None, :], weighted.reshape(count, heads, NEW, local), 0.0),
        axis=1,
    )

    def by_row(x):
        return x.reshape(count, heads, NEW).transpose(0, 2, 1).reshape(rows, heads)

    packed = jnp.concatenate(
        [
            weighted.reshape(rows, local),
            by_row(local_total),
            by_row(local_top),
            jnp.zeros((rows, 128 - 2 * heads), f32),
        ],
        axis=1,
    )
    merged = butterfly_softmax(packed, "seq", seq_masks, local, heads)
    cache_out = merged[:, :local]
    cache_total = merged[:, local : local + heads]
    cache_top = merged[:, local + heads : local + 2 * heads]

    query_all = queries.reshape(count, NEW, heads, HD)
    key_all = new_keys.reshape(count, NEW, heads, HD)
    value_all = new_values.reshape(count, NEW, heads, HD)
    fresh = jnp.einsum(
        "rthd,ruhd->rhtu", query_all, key_all, preferred_element_type=f32
    ) * HD ** (-0.5)
    causal = order[:, None] >= order[None, :]
    fresh = jnp.where(causal[None, None], fresh, NEG)
    own_top_rht = jnp.max(fresh, axis=-1)
    own_e = jnp.where(fresh > CUT, jnp.exp(fresh - own_top_rht[..., None]), 0.0)
    own_total = by_row(jnp.sum(own_e, axis=-1))
    own_out = jnp.einsum(
        "rhtu,ruhd->rthd", own_e.astype(bf16), value_all, preferred_element_type=f32
    ).reshape(rows, local)
    own_top = by_row(own_top_rht)
    top = jnp.maximum(cache_top, own_top)
    cache_scale = jnp.exp(cache_top - top)
    own_scale = jnp.exp(own_top - top)
    output = cache_out * per_column(cache_scale, local) + own_out * per_column(own_scale, local)
    total = cache_total * cache_scale + own_total * own_scale
    attn = (output / per_column(total, local)).astype(bf16)
    partial_out = jnp.dot(attn, output_weight, preferred_element_type=f32)
    mixed = butterfly_sum(partial_out, "tensor", tensor_masks)
    return (mixed, jnp.stack([keys_full, values_full]))


def solution(mesh):
    in_specs = (
        P(None, "seq"),
        P("seq"),
        P("seq", None, "tensor"),
        P("seq", None),
        P(None, "tensor"),
        P("tensor", "seq"),
        P(None, "seq", "tensor"),
        P(None, "seq", "tensor"),
        P(),
        P(),
        P(),
    )
    out_specs = (P(None, "seq"), P(None, None, "tensor"))
    seq_masks = axis_masks("seq", mesh.shape["seq"])
    tensor_masks = axis_masks("tensor", mesh.shape["tensor"])

    def body(*args):
        return shards(*args, seq_masks, tensor_masks)

    return jax.shard_map(body, mesh=mesh, in_specs=in_specs, out_specs=out_specs, check_vma=False)
```

```python
import jax
import jax.numpy as jnp
from jax import lax
from jax.sharding import PartitionSpec as P

HD = 224
NEW = 4
INPUT_WIDTH = 7168


NEG = -1e30
CUT = -1e29


def butterfly_rounds(axes):
    rounds, shift = [], 0
    for size in reversed(axes):
        masks, bit = [], 1
        while bit < size:
            masks.append((bit if 2 * bit < size or size <= 2 else size - 2 if size > 4 else size - 1) << shift)
            bit *= 2
        rounds += [tuple(masks[i : i + 2]) for i in range(0, len(masks), 2)]
        shift += size.bit_length() - 1
    return rounds


def exchange(x, axis, mask, size):
    return lax.ppermute(x, axis, [(i, i ^ mask) for i in range(size)])


def butterfly_sum(x, axis, rounds):
    size = 1 << sum(len(r) for r in rounds)
    for r in rounds:
        if len(r) == 1:
            x = x + exchange(x, axis, r[0], size)
        else:
            a, b = r
            pa, pb, pc = (exchange(x, axis, m, size) for m in (a, b, a ^ b))
            x = (x + pa) + (pb + pc)
    return x


def merge_softmax(a, b, width, heads):
    top = jnp.maximum(a[:, width + heads : width + 2 * heads], b[:, width + heads : width + 2 * heads])
    sa = jnp.exp(a[:, width + heads : width + 2 * heads] - top)
    sb = jnp.exp(b[:, width + heads : width + 2 * heads] - top)
    values = a[:, :width] * jnp.repeat(sa, HD, axis=1) + b[:, :width] * jnp.repeat(sb, HD, axis=1)
    totals = a[:, width : width + heads] * sa + b[:, width : width + heads] * sb
    pad = a.shape[1] - width - 2 * heads
    return jnp.concatenate([values, totals, top, jnp.zeros((a.shape[0], pad), jnp.float32)], axis=1)


def butterfly_softmax(x, axis, rounds, width, heads):
    size = 1 << sum(len(r) for r in rounds)
    for r in rounds:
        if len(r) == 1:
            x = merge_softmax(x, exchange(x, axis, r[0], size), width, heads)
        else:
            a, b = r
            pa, pb, pc = (exchange(x, axis, m, size) for m in (a, b, a ^ b))
            x = merge_softmax(merge_softmax(x, pa, width, heads), merge_softmax(pb, pc, width, heads), width, heads)
    return x


RINGS = {"seq": {32: (4, 8)}, "tensor": {8: (4, 2)}}


def axis_masks(axis, size):
    rings = RINGS[axis].get(size, (size,))
    return sorted(butterfly_rounds(rings), key=len)


def shards(
    features,
    input_norm_scale,
    query_key_value_weight,
    adapter_down_weight,
    adapter_up_weight,
    output_weight,
    cached_key_rows,
    cached_value_rows,
    lengths,
    sinks,
    windows,
    seq_masks,
    tensor_masks,
):
    rows = features.shape[0]
    count, span = cached_key_rows.shape[0], cached_key_rows.shape[1]
    local = adapter_up_weight.shape[1]
    heads = local // HD
    rank = adapter_down_weight.shape[1]
    f32, bf16 = jnp.float32, jnp.bfloat16

    feat = features.astype(f32)
    scaled = (feat * input_norm_scale).astype(bf16)

    def project(j):
        return jnp.dot(scaled, query_key_value_weight[:, j, :], preferred_element_type=f32)

    partial_low = jnp.dot(scaled, adapter_down_weight, preferred_element_type=f32)
    partial_sq = jnp.sum(feat * feat, axis=1, keepdims=True)
    packed = jnp.concatenate(
        [project(0), partial_low, partial_sq, jnp.zeros((rows, 127), f32)], axis=1
    )
    summed = butterfly_sum(packed, "seq", seq_masks)
    kv_summed = butterfly_sum(
        jnp.concatenate([project(1), project(2)], axis=1), "seq", [(m,) for r in seq_masks[:-1] for m in r] + seq_masks[-1:]
    )
    low = summed[:, local : local + rank]
    total_sq = summed[:, local + rank]
    scale_rows = lax.rsqrt(total_sq / INPUT_WIDTH + 1e-05)[:, None]
    lowrank = (low * scale_rows).astype(bf16)
    query_adapter = jnp.dot(lowrank, adapter_up_weight, preferred_element_type=f32)
    queries = (summed[:, :local] * scale_rows + query_adapter).astype(bf16)
    keys_full = kv_summed[:, :local] * scale_rows
    values_full = kv_summed[:, local:] * scale_rows
    new_keys = keys_full.astype(bf16)
    new_values = values_full.astype(bf16)

    col_head = jnp.arange(local, dtype=jnp.int32) // HD
    head_mask = col_head[None, :] == jnp.arange(heads, dtype=jnp.int32)[:, None]
    q_rows = queries.reshape(count, NEW, local)
    q_block = jnp.where(head_mask[None, :, None, :], q_rows[:, None, :, :], jnp.zeros((), bf16))
    q_block = q_block.reshape(count, heads * NEW, local)
    raw = jnp.einsum(
        "rnc,rpc->rnp", q_block, cached_key_rows, preferred_element_type=f32
    ) * HD ** (-0.5)
    base = lax.axis_index("seq") * span
    position = base + jnp.arange(span, dtype=jnp.int32)
    order = jnp.arange(NEW, dtype=jnp.int32)
    length = lengths[:, None, None]
    sink = sinks[:, None, None]
    window = windows[:, None, None]
    pos = position[None, None, :]
    seen = (pos < length) & ((pos < sink) | (length + order[None, :, None] - pos < window))
    seen = jnp.broadcast_to(seen[:, None], (count, heads, NEW, span)).reshape(count, heads * NEW, span)
    scores = jnp.where(seen, raw, NEG)
    local_top = jnp.max(scores, axis=-1)
    expo = jnp.where(scores > CUT, jnp.exp(scores - local_top[..., None]), 0.0)
    local_total = jnp.sum(expo, axis=-1)
    weighted = jnp.einsum(
        "rnp,rpc->rnc", expo.astype(bf16), cached_value_rows, preferred_element_type=f32
    )
    weighted = jnp.sum(
        jnp.where(head_mask[None, :, None, :], weighted.reshape(count, heads, NEW, local), 0.0),
        axis=1,
    )

    def by_row(x):
        return x.reshape(count, heads, NEW).transpose(0, 2, 1).reshape(rows, heads)

    packed = jnp.concatenate(
        [
            weighted.reshape(rows, local),
            by_row(local_total),
            by_row(local_top),
            jnp.zeros((rows, 128 - 2 * heads), f32),
        ],
        axis=1,
    )
    merged = butterfly_softmax(packed, "seq", seq_masks, local, heads)
    cache_out = merged[:, :local]
    cache_total = merged[:, local : local + heads]
    cache_top = merged[:, local + heads : local + 2 * heads]

    query_all = queries.reshape(count, NEW, heads, HD)
    key_all = new_keys.reshape(count, NEW, heads, HD)
    value_all = new_values.reshape(count, NEW, heads, HD)
    fresh = jnp.einsum(
        "rthd,ruhd->rhtu", query_all, key_all, preferred_element_type=f32
    ) * HD ** (-0.5)
    causal = order[:, None] >= order[None, :]
    fresh = jnp.where(causal[None, None], fresh, NEG)
    own_top_rht = jnp.max(fresh, axis=-1)
    own_e = jnp.where(fresh > CUT, jnp.exp(fresh - own_top_rht[..., None]), 0.0)
    own_total = by_row(jnp.sum(own_e, axis=-1))
    own_out = jnp.einsum(
        "rhtu,ruhd->rthd", own_e.astype(bf16), value_all, preferred_element_type=f32
    ).reshape(rows, local)
    own_top = by_row(own_top_rht)
    top = jnp.maximum(cache_top, own_top)
    cache_scale = jnp.exp(cache_top - top)
    own_scale = jnp.exp(own_top - top)
    output = cache_out * jnp.repeat(cache_scale, HD, axis=1) + own_out * jnp.repeat(own_scale, HD, axis=1)
    total = cache_total * cache_scale + own_total * own_scale
    attn = (output / jnp.repeat(total, HD, axis=1)).astype(bf16)
    partial_out = jnp.dot(attn, output_weight, preferred_element_type=f32)
    mixed = butterfly_sum(partial_out, "tensor", tensor_masks)
    return (mixed, jnp.stack([keys_full, values_full]))


def solution(mesh):
    in_specs = (
        P(None, "seq"),
        P("seq"),
        P("seq", None, "tensor"),
        P("seq", None),
        P(None, "tensor"),
        P("tensor", "seq"),
        P(None, "seq", "tensor"),
        P(None, "seq", "tensor"),
        P(),
        P(),
        P(),
    )
    out_specs = (P(None, "seq"), P(None, None, "tensor"))
    seq_masks = axis_masks("seq", mesh.shape["seq"])
    tensor_masks = axis_masks("tensor", mesh.shape["tensor"])

    def body(*args):
        return shards(*args, seq_masks, tensor_masks)

    return jax.shard_map(body, mesh=mesh, in_specs=in_specs, out_specs=out_specs, check_vma=False)
```
